128 devices in a mesh: dp: 16 (over y, z_lo, core), tensor: 8 (over z_hi, x).
Axes of the slice: x: 4, y: 4, z: 4 (z_hi: 2, z_lo: 2; z = z_hi * 2 + z_lo), core: 2. Of those that a mesh axis runs over, the one named last changes fastest.
Arguments:
- stream: bfloat16 [16384, 2048], P(('dp', 'tensor')), may hold values from -6 to 6
- segment: int32 [16384], P('dp'), may hold values from -1 to 16383, as said below
- position: int32 [16384], P('dp'), may hold values from 0 to 4606, as said below
- w_qkv: bfloat16 [3, 2048, 2048], P(None, 'dp', 'tensor'), may hold values from -0.5 to 0.5
- w_out: bfloat16 [2048, 2048], P('tensor', 'dp'), may hold values from -0.125 to 0.125
- w_gate_up: bfloat16 [2, 2048, 8192], P(None, 'dp', 'tensor'), may hold values from -0.125 to 0.125
- w_down: bfloat16 [8192, 2048], P('tensor', 'dp'), may hold values from -0.0625 to 0.0625
- page_table: int32 [1024], P('dp'), may hold values from 0 to 1023, as said below
Outputs:
- layer_out: bfloat16 [16384, 2048], P(('dp', 'tensor'))
- kv_cache: bfloat16 [1024, 2, 16, 2048], P('dp', None, None, 'tensor')
The draws below stay inside these ranges and needn't reach their ends.
Inputs may be any that keep to these rules, and one draw needn't show every extreme that they name: `segment`: each group's tokens form prompts of 64 to 512 tokens with distinct numbers, laid one after another, followed by padding -1 at the end of the group's stream; some prompt has 512 tokens in every group. Within a prompt positions rise by one from a first position below 4096; padding has position 0; in every group some prompt of 512 tokens starts at 4095. `page_table`: A permutation of all 1024 page ids. Among the 64 blocks of one request group, exactly 4 fall into each of the ranges o * 64 to (o + 1) * 64 - 1.
All inputs are finite; a program needn't handle non-finite values.
Results may differ from the reference program's by a relative error of at most 0.015.
Values may be sent and summed in bfloat16 or wider, within the bound.
No kernel may reach another device: no remote copies, remote signals or barrier semaphores. Data moves between devices by JAX's collectives and lax.ppermute only.
A program may use at most 128 MiB of HBM per device.

```python
import math
import jax
import jax.numpy as jnp
from jax import lax

D = 2048
HEADS = 16
HD = 128
FF = 8192
TOK_G = 1024
PAGE = 16
MIN_LEN = 64
MAX_LEN = 512
MAX_OFF = 4096
TOKENS = 16384
PAGES_G = 64
PAGES = 1024
N_DP = 16
N_TENSOR = 8


def prompt_layout(key):
    base = jax.random.fold_in(key, 11)
    count = TOK_G // MIN_LEN + 1

    def one_group(group_key):
        len_key, off_key = jax.random.split(group_key)
        lengths = jax.random.randint(len_key, (count,), MIN_LEN, MAX_LEN + 1)
        lengths = lengths.at[0].set(MAX_LEN)
        ends = jnp.cumsum(lengths)
        starts = ends - lengths
        index = jnp.arange(TOK_G)
        which = jnp.sum((index[:, None] >= ends[None, :]).astype(jnp.int32), axis=1)
        inside = ends[which] <= TOK_G
        offsets = jax.random.randint(off_key, (count,), 0, MAX_OFF)
        offsets = offsets.at[0].set(MAX_OFF - 1)
        placed = jnp.where(inside, offsets[which] + index - starts[which], 0)
        return (which, inside, placed)
    which, inside, placed = jax.vmap(one_group)(jax.random.split(base, N_DP))
    shift_by = jnp.arange(N_DP)[:, None] * TOK_G
    numbers = jnp.where(inside, which + shift_by, -1)
    return (numbers.reshape(-1).astype(jnp.int32), placed.reshape(-1).astype(jnp.int32))


def draw_segment(key, part):
    return prompt_layout(key)[0]


def draw_position(key, part):
    return prompt_layout(key)[1]


def draw_page_table(key, part):
    pages = TOK_G // PAGE
    per_owner = pages // N_DP
    owner_key, group_key = jax.random.split(jax.random.fold_in(key, 5))
    owner_pages = jax.vmap(lambda k: jax.random.permutation(k, pages))(jax.random.split(owner_key, N_DP))
    owner_pages = owner_pages + jnp.arange(N_DP)[:, None] * pages
    layout = owner_pages.reshape(N_DP, N_DP, per_owner).transpose(1, 0, 2).reshape(N_DP, pages)
    shuffle = jax.vmap(lambda k: jax.random.permutation(k, pages))(jax.random.split(group_key, N_DP))
    table = jnp.take_along_axis(layout, shuffle, axis=1)
    return table.reshape(-1).astype(jnp.int32)


def draw_stream(key, part):
    row_key = jax.random.fold_in(jax.random.fold_in(key, 3), 0)
    rows = jax.random.truncated_normal(row_key, -6.0, 6.0, (TOKENS, D), jnp.float32)
    return rows.astype(jnp.bfloat16)


def draw_w_qkv(key, part):
    base_key = jax.random.fold_in(jax.random.fold_in(key, 7), 0)
    weights = jax.random.truncated_normal(base_key, -6.0, 6.0, (3, D, D), jnp.float32) * D ** (-0.5)
    return jnp.clip(weights, -0.5, 0.5).astype(jnp.bfloat16)


def steps_of(key, extent, cuts, smallest, top_value):
    loudness = 1.0
    for axis_at, parts in cuts:
        heights = jax.random.uniform(jax.random.fold_in(jax.random.fold_in(key, 6), axis_at), (parts,), jnp.float32, smallest / len(cuts), top_value / len(cuts))
        loudness = loudness * jnp.repeat(jnp.exp(heights), extent[axis_at] // parts).reshape((-1,) + (1,) * (len(extent) - 1 - axis_at))
    return loudness


def scatter_about(key, shape, width, reach, shards=(), held_as=jnp.bfloat16):
    values = jax.random.normal(key, shape, jnp.float32) * width
    if len(shards) > 0:
        values = steps_of(key, shape, shards, -0.22, 0.18) * values
    return jnp.clip(values, min=-reach, max=reach).astype(held_as)


def setup_inputs(seed: int = 0) -> dict:
    arg_keys = jax.random.split(jax.random.key(seed), 9)
    return {
        "stream": draw_stream(jax.random.fold_in(arg_keys[8], 71), 0),
        "segment": draw_segment(jax.random.fold_in(arg_keys[8], 71), 0),
        "position": draw_position(jax.random.fold_in(arg_keys[8], 71), 0),
        "w_qkv": draw_w_qkv(jax.random.fold_in(arg_keys[8], 71), 0),
        "w_out": scatter_about(arg_keys[4], (D, D), D ** -0.5, 0.125, ((0, 8), (1, 16))),
        "w_gate_up": scatter_about(arg_keys[5], (2, D, FF), D ** -0.5, 0.125, ((1, 16), (2, 8))),
        "w_down": scatter_about(arg_keys[6], (FF, D), FF ** -0.5, 0.0625, ((0, 8), (1, 16))),
        "page_table": draw_page_table(jax.random.fold_in(arg_keys[8], 71), 0),
    }


def layer_norm(values):
    values = values.astype(jnp.float32)
    center = values - lax.optimization_barrier(jnp.mean(values, axis=-1, keepdims=True))
    spread = lax.optimization_barrier(jnp.mean(center * center, axis=-1, keepdims=True))
    return center * lax.rsqrt(spread + 1e-05)

def rotate(values, position):
    half = values.shape[-1] // 2
    freq = 10000.0 ** (-jnp.arange(half, dtype=jnp.float32) * 2.0 / values.shape[-1])
    angle = position.astype(jnp.float32)[:, None] * freq[None, :]
    cosine = jnp.cos(angle)[:, None, :]
    sine = jnp.sin(angle)[:, None, :]
    first = values[..., :half]
    second = values[..., half:]
    return jnp.concatenate([first * cosine - second * sine, second * cosine + first * sine], axis=-1)

def reference(stream, segment, position, w_qkv, w_out, w_gate_up, w_down, page_table):
    scale = 1.0 / math.sqrt(HD)
    width_t = D // N_TENSOR
    hidden_t = FF // N_TENSOR
    out_split = w_out.reshape(N_TENSOR, width_t, D).astype(jnp.float32)
    down_split = w_down.reshape(N_TENSOR, hidden_t, D).astype(jnp.float32)

    def one_group(inputs):
        rows, seg, pos = inputs
        normed = layer_norm(rows).astype(jnp.bfloat16)
        query = jnp.dot(normed, w_qkv[0], preferred_element_type=jnp.float32).reshape(TOK_G, HEADS, HD)
        keys = jnp.dot(normed, w_qkv[1], preferred_element_type=jnp.float32).reshape(TOK_G, HEADS, HD)
        values = jnp.dot(normed, w_qkv[2], preferred_element_type=jnp.float32).reshape(TOK_G, HEADS, HD)
        query = rotate(query, pos).astype(jnp.bfloat16)
        keys = rotate(keys, pos).astype(jnp.bfloat16)
        values = values.astype(jnp.bfloat16)
        scores = jnp.einsum('qhd,khd->hqk', query.astype(jnp.float32), keys.astype(jnp.float32)) * scale
        order = jnp.arange(TOK_G)
        allowed = (seg[:, None] == seg[None, :]) & (order[None, :] <= order[:, None])
        top = lax.optimization_barrier(jnp.max(jnp.where(allowed[None], scores, -1e+30), axis=-1, keepdims=True))
        weights = jnp.exp(jnp.where(allowed[None], scores - top, -1e+30))
        total = lax.optimization_barrier(jnp.sum(weights, axis=-1))
        weights_b = weights.astype(jnp.bfloat16).astype(jnp.float32)
        context = jnp.einsum('hqk,khd->qhd', weights_b, values.astype(jnp.float32))
        context = (context / jnp.transpose(total)[:, :, None]).astype(jnp.bfloat16).reshape(TOK_G, D)
        attn_terms = jnp.einsum('tsc,scd->tsd', context.reshape(TOK_G, N_TENSOR, width_t).astype(jnp.float32), out_split)
        attn_terms = lax.optimization_barrier(attn_terms.astype(jnp.bfloat16)).astype(jnp.float32)
        mid = (rows.astype(jnp.float32) + lax.optimization_barrier(jnp.sum(attn_terms, axis=1))).astype(jnp.bfloat16)
        normed2 = layer_norm(mid).astype(jnp.bfloat16)
        gate = jnp.dot(normed2, w_gate_up[0], preferred_element_type=jnp.float32)
        upward = jnp.dot(normed2, w_gate_up[1], preferred_element_type=jnp.float32)
        hidden = (jax.nn.silu(gate) * upward).astype(jnp.bfloat16)
        mlp_terms = jnp.einsum('tsc,scd->tsd', hidden.reshape(TOK_G, N_TENSOR, hidden_t).astype(jnp.float32), down_split)
        mlp_terms = lax.optimization_barrier(mlp_terms.astype(jnp.bfloat16)).astype(jnp.float32)
        result = (mid.astype(jnp.float32) + lax.optimization_barrier(jnp.sum(mlp_terms, axis=1))).astype(jnp.bfloat16)
        stacked = jnp.stack([keys.reshape(TOK_G, D), values.reshape(TOK_G, D)], axis=0)
        return (result, stacked)
    results, stacked = lax.map(one_group, (stream.reshape(N_DP, TOK_G, D), segment.reshape(N_DP, TOK_G), position.reshape(N_DP, TOK_G)))
    pages = stacked.reshape(N_DP, 2, PAGES_G, PAGE, D).transpose(0, 2, 1, 3, 4).reshape(PAGES, 2, PAGE, D)
    kv_cache = jnp.zeros((PAGES, 2, PAGE, D), jnp.bfloat16).at[page_table].set(pages)
    return (results.reshape(TOKENS, D), kv_cache)
```

```python
import math

import jax
import jax.numpy as jnp
from jax import lax
from jax.sharding import PartitionSpec as P

HD = 128


def layer_norm(values):
    values = values.astype(jnp.float32)
    center = values - jnp.mean(values, axis=-1, keepdims=True)
    spread = jnp.mean(center * center, axis=-1, keepdims=True)
    return center * lax.rsqrt(spread + 1e-05)


def rotate(values, position):
    half = values.shape[-1] // 2
    freq = 10000.0 ** (-jnp.arange(half, dtype=jnp.float32) * 2.0 / values.shape[-1])
    angle = position.astype(jnp.float32)[:, None] * freq[None, :]
    cosine = jnp.cos(angle)[:, None, :]
    sine = jnp.sin(angle)[:, None, :]
    first = values[..., :half]
    second = values[..., half:]
    return jnp.concatenate(
        [first * cosine - second * sine, second * cosine + first * sine], axis=-1
    )


def row_folder(source, piece):
    return jnp.einsum("td,cdf->ctf", source, piece, preferred_element_type=jnp.float32)


def attend(query, keys, values, segment):
    tokens = query.shape[0]
    block = min(512, tokens)
    scale = 1.0 / math.sqrt(HD)
    order = jnp.arange(tokens)
    outputs = []
    for first in range(0, tokens, block):
        last = first + block
        scores = (
            jnp.einsum(
                "qhd,khd->hqk", query[first:last], keys[:last], preferred_element_type=jnp.float32
            )
            * scale
        )
        allowed = (segment[first:last, None] == segment[None, :last]) & (
            order[None, :last] <= order[first:last, None]
        )
        top = jnp.max(jnp.where(allowed[None], scores, -1e30), axis=-1, keepdims=True)
        weights = jnp.exp(jnp.where(allowed[None], scores - top, -1e30))
        total = jnp.sum(weights, axis=-1)
        mixed = jnp.einsum(
            "hqk,khd->qhd",
            weights.astype(jnp.bfloat16),
            values[:last],
            preferred_element_type=jnp.float32,
        )
        outputs.append((mixed / jnp.transpose(total)[:, :, None]).astype(jnp.bfloat16))
    return jnp.concatenate(outputs, axis=0).reshape(tokens, -1)


def write_cache(keys, values, page_table):
    tokens = keys.shape[0]
    width = keys.shape[1] * keys.shape[2]
    pages = page_table.shape[0]
    page_size = tokens // pages
    owners = lax.axis_size("dp")
    per_owner = pages // owners
    stacked = jnp.stack([keys.reshape(tokens, width), values.reshape(tokens, width)], axis=0)
    stacked = stacked.reshape(2, pages, page_size, width).transpose(1, 0, 2, 3)
    order = jnp.argsort(page_table // pages, stable=True)
    outgoing = stacked[order].reshape(owners, per_owner, 2, page_size, width)
    outgoing_ids = page_table[order].reshape(owners, per_owner)
    arrived, arrived_ids = (
        lax.all_to_all(outgoing, "dp", split_axis=0, concat_axis=0, tiled=True),
        lax.all_to_all(outgoing_ids, "dp", split_axis=0, concat_axis=0, tiled=True),
    )
    local = (arrived_ids - lax.axis_index("dp") * pages).reshape(-1)
    empty = jnp.zeros((pages, 2, page_size, width), jnp.bfloat16)
    return empty.at[local].set(arrived.reshape(pages, 2, page_size, width))


def gather_packed(pieces, axis_name):
    rows = [piece.shape[0] for piece in pieces]
    packed = jnp.concatenate(pieces, axis=0)
    gathered = lax.all_gather(packed, axis_name, axis=0, tiled=False)
    outputs, first = [], 0
    for count in rows:
        outputs.append(gathered[:, first:first + count])
        first += count
    return outputs


def body(stream, segment, position, w_qkv, w_out, w_gate_up, w_down, page_table):
    tok_group = segment.shape[0]
    share_rows = stream.shape[0]
    owners = lax.axis_size("dp")
    width = w_qkv.shape[1]
    local_cols = w_qkv.shape[2]
    hidden_cols = w_gate_up.shape[2]
    qkv_g, out_g = gather_packed(
        [w_qkv.reshape(3 * width, local_cols), jnp.transpose(w_out)], "dp"
    )
    qkv_g = qkv_g.reshape(owners, 3, width, local_cols)
    gu_g, down_g = gather_packed(
        [w_gate_up.reshape(2 * width, hidden_cols), jnp.transpose(w_down)], "dp"
    )
    gu_g = gu_g.reshape(owners, 2, width, hidden_cols)
    full_stream = lax.all_gather(stream, "tensor", axis=0, tiled=True)
    normed = layer_norm(full_stream).astype(jnp.bfloat16).reshape(tok_group, owners, width)
    local_heads = local_cols // HD
    projected = jnp.einsum("tgd,gcdf->ctf", normed, qkv_g, preferred_element_type=jnp.float32)
    query = rotate(projected[0].reshape(tok_group, local_heads, HD), position).astype(jnp.bfloat16)
    keys = rotate(projected[1].reshape(tok_group, local_heads, HD), position).astype(jnp.bfloat16)
    values = projected[2].reshape(tok_group, local_heads, HD).astype(jnp.bfloat16)
    context = attend(query, keys, values, segment)
    attn_part = jnp.einsum(
        "tr,gcr->tgc", context, out_g, preferred_element_type=jnp.float32
    ).reshape(tok_group, owners * width)
    attn_part, gu_g, down_g = lax.optimization_barrier((attn_part, gu_g, down_g))
    attn_whole = lax.psum(attn_part.astype(jnp.bfloat16), "tensor").astype(jnp.float32)
    mid = (full_stream.astype(jnp.float32) + attn_whole).astype(jnp.bfloat16)
    normed2 = layer_norm(mid).astype(jnp.bfloat16).reshape(tok_group, owners, width)
    gate_up = jnp.einsum("tgd,gcdf->ctf", normed2, gu_g, preferred_element_type=jnp.float32)
    hidden = (jax.nn.silu(gate_up[0]) * gate_up[1]).astype(jnp.bfloat16)
    mlp_part = jnp.einsum(
        "tf,gcf->tgc", hidden, down_g, preferred_element_type=jnp.float32
    ).reshape(tok_group, owners * width)
    mlp_mine = lax.psum_scatter(
        mlp_part.astype(jnp.bfloat16), "tensor", scatter_dimension=0, tiled=True
    ).astype(jnp.float32)
    mid_mine = lax.dynamic_slice_in_dim(mid, lax.axis_index("tensor") * share_rows, share_rows, 0)
    layer_out = (mid_mine.astype(jnp.float32) + mlp_mine).astype(jnp.bfloat16)
    kv_cache = write_cache(keys, values, page_table)
    return (layer_out, kv_cache)


def solution(mesh):
    return jax.shard_map(
        body,
        mesh=mesh,
        in_specs=(
            P(("dp", "tensor"), None),
            P("dp"),
            P("dp"),
            P(None, "dp", "tensor"),
            P("tensor", "dp"),
            P(None, "dp", "tensor"),
            P("tensor", "dp"),
            P("dp"),
        ),
        out_specs=(P(("dp", "tensor"), None), P("dp", None, None, "tensor")),
        check_vma=False,
    )
```

```python
import math

import jax
import jax.numpy as jnp
from jax import lax
from jax.sharding import PartitionSpec as P

HD = 128


def layer_norm(values):
    values = values.astype(jnp.float32)
    center = values - jnp.mean(values, axis=-1, keepdims=True)
    spread = jnp.mean(center * center, axis=-1, keepdims=True)
    return center * lax.rsqrt(spread + 1e-05)


def rotate(values, position):
    half = values.shape[-1] // 2
    freq = 10000.0 ** (-jnp.arange(half, dtype=jnp.float32) * 2.0 / values.shape[-1])
    angle = position.astype(jnp.float32)[:, None] * freq[None, :]
    cosine = jnp.cos(angle)[:, None, :]
    sine = jnp.sin(angle)[:, None, :]
    first = values[..., :half]
    second = values[..., half:]
    return jnp.concatenate(
        [first * cosine - second * sine, second * cosine + first * sine], axis=-1
    )


def row_folder(source, piece):
    return jnp.einsum("td,cdf->ctf", source, piece, preferred_element_type=jnp.float32)


def attend(query, keys, values, segment):
    tokens = query.shape[0]
    block = min(512, tokens)
    scale = 1.0 / math.sqrt(HD)
    order = jnp.arange(tokens)
    outputs = []
    for first in range(0, tokens, block):
        last = first + block
        scores = (
            jnp.einsum(
                "qhd,khd->hqk", query[first:last], keys[:last], preferred_element_type=jnp.float32
            )
            * scale
        )
        allowed = (segment[first:last, None] == segment[None, :last]) & (
            order[None, :last] <= order[first:last, None]
        )
        top = jnp.max(jnp.where(allowed[None], scores, -1e30), axis=-1, keepdims=True)
        weights = jnp.exp(jnp.where(allowed[None], scores - top, -1e30))
        total = jnp.sum(weights, axis=-1)
        mixed = jnp.einsum(
            "hqk,khd->qhd",
            weights.astype(jnp.bfloat16),
            values[:last],
            preferred_element_type=jnp.float32,
        )
        outputs.append((mixed / jnp.transpose(total)[:, :, None]).astype(jnp.bfloat16))
    return jnp.concatenate(outputs, axis=0).reshape(tokens, -1)


def write_cache(keys, values, page_table):
    tokens = keys.shape[0]
    width = keys.shape[1] * keys.shape[2]
    pages = page_table.shape[0]
    page_size = tokens // pages
    owners = lax.axis_size("dp")
    per_owner = pages // owners
    stacked = jnp.stack([keys.reshape(tokens, width), values.reshape(tokens, width)], axis=0)
    stacked = stacked.reshape(2, pages, page_size, width).transpose(1, 0, 2, 3)
    order = jnp.argsort(page_table // pages, stable=True)
    outgoing = stacked[order].reshape(owners, per_owner, 2, page_size, width)
    outgoing_ids = page_table[order].reshape(owners, per_owner)
    arrived, arrived_ids = (
        lax.all_to_all(outgoing, "dp", split_axis=0, concat_axis=0, tiled=True),
        lax.all_to_all(outgoing_ids, "dp", split_axis=0, concat_axis=0, tiled=True),
    )
    local = (arrived_ids - lax.axis_index("dp") * pages).reshape(-1)
    empty = jnp.zeros((pages, 2, page_size, width), jnp.bfloat16)
    return empty.at[local].set(arrived.reshape(pages, 2, page_size, width))


def gather_packed(pieces, axis_name):
    rows = [piece.shape[0] for piece in pieces]
    packed = jnp.concatenate(pieces, axis=0)
    gathered = lax.all_gather(packed, axis_name, axis=0, tiled=False)
    outputs, first = [], 0
    for count in rows:
        outputs.append(gathered[:, first:first + count])
        first += count
    return outputs


def gather_rows(rows, axis_name):
    count = lax.axis_size(axis_name)
    copies = jnp.broadcast_to(rows[None], (count,) + rows.shape)
    gathered = lax.all_to_all(copies, axis_name, 0, 0, tiled=True)
    return gathered.reshape(count * rows.shape[0], rows.shape[1])


def sum_rows(terms, axis_name):
    count = lax.axis_size(axis_name)
    arrived = lax.all_to_all(
        terms.reshape(count, terms.shape[0] // count, terms.shape[1]), axis_name, 0, 0, tiled=True
    )
    return jnp.sum(arrived.astype(jnp.float32), axis=0)


def body(stream, segment, position, w_qkv, w_out, w_gate_up, w_down, page_table):
    tok_group = segment.shape[0]
    owners = lax.axis_size("dp")
    width = w_qkv.shape[1]
    local_cols = w_qkv.shape[2]
    hidden_cols = w_gate_up.shape[2]
    qkv_g, out_g = gather_packed(
        [w_qkv.reshape(3 * width, local_cols), jnp.transpose(w_out)], "dp"
    )
    qkv_g = qkv_g.reshape(owners, 3, width, local_cols)
    gu_g, down_g = gather_packed(
        [w_gate_up.reshape(2 * width, hidden_cols), jnp.transpose(w_down)], "dp"
    )
    gu_g = gu_g.reshape(owners, 2, width, hidden_cols)
    full_stream = gather_rows(stream, "tensor")
    normed = layer_norm(full_stream).astype(jnp.bfloat16).reshape(tok_group, owners, width)
    local_heads = local_cols // HD
    projected = jnp.einsum("tgd,gcdf->ctf", normed, qkv_g, preferred_element_type=jnp.float32)
    query = rotate(projected[0].reshape(tok_group, local_heads, HD), position).astype(jnp.bfloat16)
    keys = rotate(projected[1].reshape(tok_group, local_heads, HD), position).astype(jnp.bfloat16)
    values = projected[2].reshape(tok_group, local_heads, HD).astype(jnp.bfloat16)
    context = attend(query, keys, values, segment)
    attn_part = jnp.einsum(
        "tr,gcr->tgc", context, out_g, preferred_element_type=jnp.float32
    ).reshape(tok_group, owners * width)
    attn_mine = sum_rows(attn_part.astype(jnp.bfloat16), "tensor")
    mid = (stream.astype(jnp.float32) + attn_mine).astype(jnp.bfloat16)
    normed2_mine = layer_norm(mid).astype(jnp.bfloat16)
    normed2 = gather_rows(normed2_mine, "tensor").reshape(tok_group, owners, width)
    gate_up = jnp.einsum("tgd,gcdf->ctf", normed2, gu_g, preferred_element_type=jnp.float32)
    hidden = (jax.nn.silu(gate_up[0]) * gate_up[1]).astype(jnp.bfloat16)
    mlp_part = jnp.einsum(
        "tf,gcf->tgc", hidden, down_g, preferred_element_type=jnp.float32
    ).reshape(tok_group, owners * width)
    mlp_mine = sum_rows(mlp_part.astype(jnp.bfloat16), "tensor")
    layer_out = (mid.astype(jnp.float32) + mlp_mine).astype(jnp.bfloat16)
    kv_cache = write_cache(keys, values, page_table)
    return (layer_out, kv_cache)


def solution(mesh):
    return jax.shard_map(
        body,
        mesh=mesh,
        in_specs=(
            P(("dp", "tensor"), None),
            P("dp"),
            P("dp"),
            P(None, "dp", "tensor"),
            P("tensor", "dp"),
            P(None, "dp", "tensor"),
            P("tensor", "dp"),
            P("dp"),
        ),
        out_specs=(P(("dp", "tensor"), None), P("dp", None, None, "tensor")),
        check_vma=False,
    )
```

```python
import math

import jax
import jax.numpy as jnp
from jax import lax
from jax.sharding import PartitionSpec as P

HD = 128


def layer_norm(values):
    values = values.astype(jnp.float32)
    center = values - jnp.mean(values, axis=-1, keepdims=True)
    spread = jnp.mean(center * center, axis=-1, keepdims=True)
    return center * lax.rsqrt(spread + 1e-05)


def rotate(values, position):
    half = values.shape[-1] // 2
    freq = 10000.0 ** (-jnp.arange(half, dtype=jnp.float32) * 2.0 / values.shape[-1])
    angle = position.astype(jnp.float32)[:, None] * freq[None, :]
    cosine = jnp.cos(angle)[:, None, :]
    sine = jnp.sin(angle)[:, None, :]
    first = values[..., :half]
    second = values[..., half:]
    return jnp.concatenate(
        [first * cosine - second * sine, second * cosine + first * sine], axis=-1
    )


def row_folder(source, piece):
    return jnp.einsum("td,cdf->ctf", source, piece, preferred_element_type=jnp.float32)


def attend(query, keys, values, segment):
    tokens = query.shape[0]
    block = min(512, tokens)
    scale = 1.0 / math.sqrt(HD)
    order = jnp.arange(tokens)
    outputs = []
    for first in range(0, tokens, block):
        last = first + block
        scores = (
            jnp.einsum(
                "qhd,khd->hqk", query[first:last], keys[:last], preferred_element_type=jnp.float32
            )
            * scale
        )
        allowed = (segment[first:last, None] == segment[None, :last]) & (
            order[None, :last] <= order[first:last, None]
        )
        top = jnp.max(jnp.where(allowed[None], scores, -1e30), axis=-1, keepdims=True)
        weights = jnp.exp(jnp.where(allowed[None], scores - top, -1e30))
        total = jnp.sum(weights, axis=-1)
        mixed = jnp.einsum(
            "hqk,khd->qhd",
            weights.astype(jnp.bfloat16),
            values[:last],
            preferred_element_type=jnp.float32,
        )
        outputs.append((mixed / jnp.transpose(total)[:, :, None]).astype(jnp.bfloat16))
    return jnp.concatenate(outputs, axis=0).reshape(tokens, -1)


def write_cache(keys, values, page_table):
    tokens = keys.shape[0]
    width = keys.shape[1] * keys.shape[2]
    pages = page_table.shape[0]
    page_size = tokens // pages
    owners = lax.axis_size("dp")
    per_owner = pages // owners
    stacked = jnp.stack([keys.reshape(tokens, width), values.reshape(tokens, width)], axis=0)
    stacked = stacked.reshape(2, pages, page_size, width).transpose(1, 0, 2, 3)
    order = jnp.argsort(page_table // pages, stable=True)
    outgoing = stacked[order].reshape(owners, per_owner, 2, page_size, width)
    outgoing_ids = page_table[order].reshape(owners, per_owner)
    arrived, arrived_ids = (
        lax.all_to_all(outgoing, "dp", split_axis=0, concat_axis=0, tiled=True),
        lax.all_to_all(outgoing_ids, "dp", split_axis=0, concat_axis=0, tiled=True),
    )
    local = (arrived_ids - lax.axis_index("dp") * pages).reshape(-1)
    empty = jnp.zeros((pages, 2, page_size, width), jnp.bfloat16)
    return empty.at[local].set(arrived.reshape(pages, 2, page_size, width))


def gather_packed(pieces, axis_name):
    rows = [piece.shape[0] for piece in pieces]
    packed = jnp.concatenate(pieces, axis=0)
    gathered = lax.all_gather(packed, axis_name, axis=0, tiled=False)
    outputs, first = [], 0
    for count in rows:
        outputs.append(gathered[:, first:first + count])
        first += count
    return outputs


def gather_rows(rows, axis_name):
    count = lax.axis_size(axis_name)
    copies = jnp.broadcast_to(rows[None], (count,) + rows.shape)
    gathered = lax.all_to_all(copies, axis_name, 0, 0, tiled=True)
    return gathered.reshape(count * rows.shape[0], rows.shape[1])


def sum_rows(terms, axis_name):
    count = lax.axis_size(axis_name)
    arrived = lax.all_to_all(
        terms.reshape(count, terms.shape[0] // count, terms.shape[1]), axis_name, 0, 0, tiled=True
    )
    return jnp.sum(arrived.astype(jnp.float32), axis=0)


def body(stream, segment, position, w_qkv, w_out, w_gate_up, w_down, page_table):
    tok_group = segment.shape[0]
    share_rows = stream.shape[0]
    local_cols = w_qkv.shape[2]
    attn_w = lax.all_gather(
        jnp.concatenate([w_qkv, jnp.transpose(w_out)[None]], axis=0), "dp", axis=1, tiled=True
    )
    mlp_w = lax.all_gather(
        jnp.concatenate([w_gate_up, jnp.transpose(w_down)[None]], axis=0), "dp", axis=1, tiled=True
    )
    full_stream = gather_rows(stream, "tensor")
    normed = layer_norm(full_stream).astype(jnp.bfloat16)
    local_heads = local_cols // HD
    projected = jnp.einsum("td,cdf->ctf", normed, attn_w[:3], preferred_element_type=jnp.float32)
    query = rotate(projected[0].reshape(tok_group, local_heads, HD), position).astype(jnp.bfloat16)
    keys = rotate(projected[1].reshape(tok_group, local_heads, HD), position).astype(jnp.bfloat16)
    values = projected[2].reshape(tok_group, local_heads, HD).astype(jnp.bfloat16)
    context = attend(query, keys, values, segment)
    attn_part = jnp.einsum("tr,dr->td", context, attn_w[3], preferred_element_type=jnp.float32)
    attn_mine = sum_rows(attn_part.astype(jnp.bfloat16), "tensor")
    mid = (stream.astype(jnp.float32) + attn_mine).astype(jnp.bfloat16)
    normed2_mine = layer_norm(mid).astype(jnp.bfloat16)
    pieces = 2
    piece = share_rows // pieces
    mlp_pieces = []
    for first in range(0, share_rows, piece):
        rows = gather_rows(normed2_mine[first:first + piece], "tensor")
        gate_up = jnp.einsum("td,cdf->ctf", rows, mlp_w[:2], preferred_element_type=jnp.float32)
        hidden = (jax.nn.silu(gate_up[0]) * gate_up[1]).astype(jnp.bfloat16)
        mlp_part = jnp.einsum("tf,df->td", hidden, mlp_w[2], preferred_element_type=jnp.float32)
        mlp_pieces.append(sum_rows(mlp_part.astype(jnp.bfloat16), "tensor"))
    mlp_mine = jnp.concatenate(mlp_pieces, axis=0)
    layer_out = (mid.astype(jnp.float32) + mlp_mine).astype(jnp.bfloat16)
    kv_cache = write_cache(keys, values, page_table)
    return (layer_out, kv_cache)


def solution(mesh):
    return jax.shard_map(
        body,
        mesh=mesh,
        in_specs=(
            P(("dp", "tensor"), None),
            P("dp"),
            P("dp"),
            P(None, "dp", "tensor"),
            P("tensor", "dp"),
            P(None, "dp", "tensor"),
            P("tensor", "dp"),
            P("dp"),
        ),
        out_specs=(P(("dp", "tensor"), None), P("dp", None, None, "tensor")),
        check_vma=False,
    )
```

```python
import math

import numpy as np

import jax
import jax.numpy as jnp
from jax import lax
from jax.sharding import PartitionSpec as P

HD = 128


def layer_norm(values):
    values = values.astype(jnp.float32)
    center = values - jnp.mean(values, axis=-1, keepdims=True)
    spread = jnp.mean(center * center, axis=-1, keepdims=True)
    return center * lax.rsqrt(spread + 1e-05)


def rotate(values, position):
    half = values.shape[-1] // 2
    freq = 10000.0 ** (-jnp.arange(half, dtype=jnp.float32) * 2.0 / values.shape[-1])
    angle = position.astype(jnp.float32)[:, None] * freq[None, :]
    cosine = jnp.cos(angle)[:, None, :]
    sine = jnp.sin(angle)[:, None, :]
    first = values[..., :half]
    second = values[..., half:]
    return jnp.concatenate(
        [first * cosine - second * sine, second * cosine + first * sine], axis=-1
    )


def row_folder(source, piece):
    return jnp.einsum("td,cdf->ctf", source, piece, preferred_element_type=jnp.float32)


def attend(query, keys, values, segment):
    tokens = query.shape[0]
    block = min(512, tokens)
    scale = 1.0 / math.sqrt(HD)
    order = jnp.arange(tokens)
    outputs = []
    for first in range(0, tokens, block):
        last = first + block
        scores = (
            jnp.einsum(
                "qhd,khd->hqk", query[first:last], keys[:last], preferred_element_type=jnp.float32
            )
            * scale
        )
        allowed = (segment[first:last, None] == segment[None, :last]) & (
            order[None, :last] <= order[first:last, None]
        )
        top = jnp.max(jnp.where(allowed[None], scores, -1e30), axis=-1, keepdims=True)
        weights = jnp.exp(jnp.where(allowed[None], scores - top, -1e30))
        total = jnp.sum(weights, axis=-1)
        mixed = jnp.einsum(
            "hqk,khd->qhd",
            weights.astype(jnp.bfloat16),
            values[:last],
            preferred_element_type=jnp.float32,
        )
        outputs.append((mixed / jnp.transpose(total)[:, :, None]).astype(jnp.bfloat16))
    return jnp.concatenate(outputs, axis=0).reshape(tokens, -1)


def write_cache(keys, values, page_table):
    tokens = keys.shape[0]
    width = keys.shape[1] * keys.shape[2]
    pages = page_table.shape[0]
    page_size = tokens // pages
    owners = lax.axis_size("dp")
    per_owner = pages // owners
    stacked = jnp.stack([keys.reshape(tokens, width), values.reshape(tokens, width)], axis=0)
    stacked = stacked.reshape(2, pages, page_size, width).transpose(1, 0, 2, 3)
    order = jnp.argsort(page_table // pages, stable=True)
    outgoing = stacked[order].reshape(owners, per_owner, 2, page_size, width)
    outgoing_ids = page_table[order].reshape(owners, per_owner)
    arrived, arrived_ids = (
        lax.all_to_all(outgoing, "dp", split_axis=0, concat_axis=0, tiled=True),
        lax.all_to_all(outgoing_ids, "dp", split_axis=0, concat_axis=0, tiled=True),
    )
    local = (arrived_ids - lax.axis_index("dp") * pages).reshape(-1)
    empty = jnp.zeros((pages, 2, page_size, width), jnp.bfloat16)
    return empty.at[local].set(arrived.reshape(pages, 2, page_size, width))


def gather_packed(pieces, axis_name):
    rows = [piece.shape[0] for piece in pieces]
    packed = jnp.concatenate(pieces, axis=0)
    gathered = lax.all_gather(packed, axis_name, axis=0, tiled=False)
    outputs, first = [], 0
    for count in rows:
        outputs.append(gathered[:, first:first + count])
        first += count
    return outputs


def gather_rows(rows, axis_name):
    count = lax.axis_size(axis_name)
    copies = jnp.broadcast_to(rows[None], (count,) + rows.shape)
    gathered = lax.all_to_all(copies, axis_name, 0, 0, tiled=True)
    return gathered.reshape(count * rows.shape[0], rows.shape[1])


def sum_rows(terms, axis_name):
    count = lax.axis_size(axis_name)
    arrived = lax.all_to_all(
        terms.reshape(count, terms.shape[0] // count, terms.shape[1]), axis_name, 0, 0, tiled=True
    )
    return jnp.sum(arrived.astype(jnp.float32), axis=0)


def attend_block(query, keys, values, seg_q, seg_k, q_index):
    scale = 1.0 / math.sqrt(HD)
    scores = (
        jnp.einsum("qhd,khd->hqk", query, keys, preferred_element_type=jnp.float32) * scale
    )
    allowed = (seg_q[:, None] == seg_k[None, :]) & (
        jnp.arange(keys.shape[0])[None, :] <= jnp.asarray(q_index)[:, None]
    )
    top = jnp.max(jnp.where(allowed[None], scores, -1e30), axis=-1, keepdims=True)
    weights = jnp.exp(jnp.where(allowed[None], scores - top, -1e30))
    total = jnp.sum(weights, axis=-1)
    mixed = jnp.einsum(
        "hqk,khd->qhd", weights.astype(jnp.bfloat16), values, preferred_element_type=jnp.float32
    )
    mixed = (mixed / jnp.transpose(total)[:, :, None]).astype(jnp.bfloat16)
    return mixed.reshape(query.shape[0], -1)


def body(stream, segment, position, w_qkv, w_out, w_gate_up, w_down, page_table):
    tok_group = segment.shape[0]
    share_rows = stream.shape[0]
    shares = tok_group // share_rows
    local_cols = w_qkv.shape[2]
    attn_w = lax.all_gather(
        jnp.concatenate([w_qkv, jnp.transpose(w_out)[None]], axis=0), "dp", axis=1, tiled=True
    )
    mlp_w = lax.all_gather(
        jnp.concatenate([w_gate_up, jnp.transpose(w_down)[None]], axis=0), "dp", axis=1, tiled=True
    )
    full_stream = gather_rows(stream, "tensor")
    normed = layer_norm(full_stream).astype(jnp.bfloat16)
    local_heads = local_cols // HD
    projected = jnp.einsum("td,cdf->ctf", normed, attn_w[:3], preferred_element_type=jnp.float32)
    query = rotate(projected[0].reshape(tok_group, local_heads, HD), position).astype(jnp.bfloat16)
    keys = rotate(projected[1].reshape(tok_group, local_heads, HD), position).astype(jnp.bfloat16)
    values = projected[2].reshape(tok_group, local_heads, HD).astype(jnp.bfloat16)
    kv_cache = write_cache(keys, values, page_table)

    pieces = 2
    piece = share_rows // pieces
    span = 2
    query_grid = query.reshape(shares, pieces, piece, local_heads, HD)
    segment_grid = segment.reshape(shares, pieces, piece)
    index_grid = np.arange(tok_group).reshape(shares, pieces, piece)
    outputs = []
    for p in range(pieces):
        blocks = []
        for s in range(0, shares, span):
            k_len = (s + span) * share_rows
            blocks.append(
                attend_block(
                    query_grid[s:s + span, p].reshape(span * piece, local_heads, HD),
                    keys[:k_len],
                    values[:k_len],
                    segment_grid[s:s + span, p].reshape(span * piece),
                    segment[:k_len],
                    index_grid[s:s + span, p].reshape(span * piece),
                )
            )
        context = jnp.concatenate(blocks, axis=0)
        attn_part = jnp.einsum("tr,dr->td", context, attn_w[3], preferred_element_type=jnp.float32)
        attn_mine = sum_rows(attn_part.astype(jnp.bfloat16), "tensor")
        mid = (stream[p * piece:(p + 1) * piece].astype(jnp.float32) + attn_mine).astype(
            jnp.bfloat16
        )
        rows = gather_rows(layer_norm(mid).astype(jnp.bfloat16), "tensor")
        gate_up = jnp.einsum("td,cdf->ctf", rows, mlp_w[:2], preferred_element_type=jnp.float32)
        hidden = (jax.nn.silu(gate_up[0]) * gate_up[1]).astype(jnp.bfloat16)
        mlp_part = jnp.einsum("tf,df->td", hidden, mlp_w[2], preferred_element_type=jnp.float32)
        mlp_mine = sum_rows(mlp_part.astype(jnp.bfloat16), "tensor")
        outputs.append((mid.astype(jnp.float32) + mlp_mine).astype(jnp.bfloat16))
    layer_out = jnp.concatenate(outputs, axis=0)
    return (layer_out, kv_cache)


def solution(mesh):
    return jax.shard_map(
        body,
        mesh=mesh,
        in_specs=(
            P(("dp", "tensor"), None),
            P("dp"),
            P("dp"),
            P(None, "dp", "tensor"),
            P("tensor", "dp"),
            P(None, "dp", "tensor"),
            P("tensor", "dp"),
            P("dp"),
        ),
        out_specs=(P(("dp", "tensor"), None), P("dp", None, None, "tensor")),
        check_vma=False,
    )
```

```python
import math

import numpy as np

import jax
import jax.numpy as jnp
from jax import lax
from jax.sharding import PartitionSpec as P

HD = 128


def layer_norm(values):
    values = values.astype(jnp.float32)
    center = values - jnp.mean(values, axis=-1, keepdims=True)
    spread = jnp.mean(center * center, axis=-1, keepdims=True)
    return center * lax.rsqrt(spread + 1e-05)


def rotate(values, position):
    half = values.shape[-1] // 2
    freq = 10000.0 ** (-jnp.arange(half, dtype=jnp.float32) * 2.0 / values.shape[-1])
    angle = position.astype(jnp.float32)[:, None] * freq[None, :]
    cosine = jnp.cos(angle)[:, None, :]
    sine = jnp.sin(angle)[:, None, :]
    first = values[..., :half]
    second = values[..., half:]
    return jnp.concatenate(
        [first * cosine - second * sine, second * cosine + first * sine], axis=-1
    )


def row_folder(source, piece):
    return jnp.einsum("td,cdf->ctf", source, piece, preferred_element_type=jnp.float32)


def attend(query, keys, values, segment):
    tokens = query.shape[0]
    block = min(512, tokens)
    scale = 1.0 / math.sqrt(HD)
    order = jnp.arange(tokens)
    outputs = []
    for first in range(0, tokens, block):
        last = first + block
        scores = (
            jnp.einsum(
                "qhd,khd->hqk", query[first:last], keys[:last], preferred_element_type=jnp.float32
            )
            * scale
        )
        allowed = (segment[first:last, None] == segment[None, :last]) & (
            order[None, :last] <= order[first:last, None]
        )
        top = jnp.max(jnp.where(allowed[None], scores, -1e30), axis=-1, keepdims=True)
        weights = jnp.exp(jnp.where(allowed[None], scores - top, -1e30))
        total = jnp.sum(weights, axis=-1)
        mixed = jnp.einsum(
            "hqk,khd->qhd",
            weights.astype(jnp.bfloat16),
            values[:last],
            preferred_element_type=jnp.float32,
        )
        outputs.append((mixed / jnp.transpose(total)[:, :, None]).astype(jnp.bfloat16))
    return jnp.concatenate(outputs, axis=0).reshape(tokens, -1)


def write_cache(keys, values, page_table):
    tokens = keys.shape[0]
    width = keys.shape[1] * keys.shape[2]
    pages = page_table.shape[0]
    page_size = tokens // pages
    owners = lax.axis_size("dp")
    per_owner = pages // owners
    stacked = jnp.stack([keys.reshape(tokens, width), values.reshape(tokens, width)], axis=0)
    stacked = stacked.reshape(2, pages, page_size, width).transpose(1, 0, 2, 3)
    order = jnp.argsort(page_table // pages, stable=True)
    outgoing = stacked[order].reshape(owners, per_owner, 2, page_size, width)
    outgoing_ids = page_table[order].reshape(owners, per_owner)
    arrived, arrived_ids = (
        lax.all_to_all(outgoing, "dp", split_axis=0, concat_axis=0, tiled=True),
        lax.all_to_all(outgoing_ids, "dp", split_axis=0, concat_axis=0, tiled=True),
    )
    local = (arrived_ids - lax.axis_index("dp") * pages).reshape(-1)
    empty = jnp.zeros((pages, 2, page_size, width), jnp.bfloat16)
    return empty.at[local].set(arrived.reshape(pages, 2, page_size, width))


def gather_packed(pieces, axis_name):
    rows = [piece.shape[0] for piece in pieces]
    packed = jnp.concatenate(pieces, axis=0)
    gathered = lax.all_gather(packed, axis_name, axis=0, tiled=False)
    outputs, first = [], 0
    for count in rows:
        outputs.append(gathered[:, first:first + count])
        first += count
    return outputs


def gather_rows(rows, axis_name):
    count = lax.axis_size(axis_name)
    copies = jnp.broadcast_to(rows[None], (count,) + rows.shape)
    gathered = lax.all_to_all(copies, axis_name, 0, 0, tiled=True)
    return gathered.reshape(count * rows.shape[0], rows.shape[1])


def sum_rows(terms, axis_name):
    count = lax.axis_size(axis_name)
    arrived = lax.all_to_all(
        terms.reshape(count, terms.shape[0] // count, terms.shape[1]), axis_name, 0, 0, tiled=True
    )
    return jnp.sum(arrived.astype(jnp.float32), axis=0)


def attend_block(query, keys, values, seg_q, seg_k, q_index):
    scale = 1.0 / math.sqrt(HD)
    scores = (
        jnp.einsum("qhd,khd->hqk", query, keys, preferred_element_type=jnp.float32) * scale
    )
    allowed = (seg_q[:, None] == seg_k[None, :]) & (
        jnp.arange(keys.shape[0])[None, :] <= jnp.asarray(q_index)[:, None]
    )
    top = jnp.max(jnp.where(allowed[None], scores, -1e30), axis=-1, keepdims=True)
    weights = jnp.exp(jnp.where(allowed[None], scores - top, -1e30))
    total = jnp.sum(weights, axis=-1)
    mixed = jnp.einsum(
        "hqk,khd->qhd", weights.astype(jnp.bfloat16), values, preferred_element_type=jnp.float32
    )
    mixed = (mixed / jnp.transpose(total)[:, :, None]).astype(jnp.bfloat16)
    return mixed.reshape(query.shape[0], -1)


def body(stream, segment, position, w_qkv, w_out, w_gate_up, w_down, page_table):
    tok_group = segment.shape[0]
    share_rows = stream.shape[0]
    shares = tok_group // share_rows
    local_cols = w_qkv.shape[2]
    attn_w = lax.all_gather(
        jnp.concatenate([w_qkv, jnp.transpose(w_out)[None]], axis=0), "dp", axis=1, tiled=True
    )
    mlp_w = lax.all_gather(
        jnp.concatenate([w_gate_up, jnp.transpose(w_down)[None]], axis=0), "dp", axis=1, tiled=True
    )
    full_stream = gather_rows(stream, "tensor")
    normed = layer_norm(full_stream).astype(jnp.bfloat16)
    local_heads = local_cols // HD
    projected = jnp.einsum("td,cdf->ctf", normed, attn_w[:3], preferred_element_type=jnp.float32)
    query = rotate(projected[0].reshape(tok_group, local_heads, HD), position).astype(jnp.bfloat16)
    keys = rotate(projected[1].reshape(tok_group, local_heads, HD), position).astype(jnp.bfloat16)
    values = projected[2].reshape(tok_group, local_heads, HD).astype(jnp.bfloat16)
    kv_cache = write_cache(keys, values, page_table)

    pieces = 2
    piece = share_rows // pieces
    span = 2
    query_grid = query.reshape(shares, pieces, piece, local_heads, HD)
    segment_grid = segment.reshape(shares, pieces, piece)
    index_grid = np.arange(tok_group).reshape(shares, pieces, piece)

    def attention_piece(p):
        blocks = []
        for s in range(0, shares, span):
            k_len = (s + span) * share_rows
            blocks.append(
                attend_block(
                    query_grid[s:s + span, p].reshape(span * piece, local_heads, HD),
                    keys[:k_len],
                    values[:k_len],
                    segment_grid[s:s + span, p].reshape(span * piece),
                    segment[:k_len],
                    index_grid[s:s + span, p].reshape(span * piece),
                )
            )
        context = jnp.concatenate(blocks, axis=0)
        attn_part = jnp.einsum("tr,dr->td", context, attn_w[3], preferred_element_type=jnp.float32)
        return attn_part.astype(jnp.bfloat16)

    def mid_of(p, attn_part):
        attn_mine = sum_rows(attn_part, "tensor")
        mid = (stream[p * piece:(p + 1) * piece].astype(jnp.float32) + attn_mine).astype(
            jnp.bfloat16
        )
        return mid, gather_rows(layer_norm(mid).astype(jnp.bfloat16), "tensor")

    def mlp_of(rows):
        gate_up = jnp.einsum("td,cdf->ctf", rows, mlp_w[:2], preferred_element_type=jnp.float32)
        hidden = (jax.nn.silu(gate_up[0]) * gate_up[1]).astype(jnp.bfloat16)
        mlp_part = jnp.einsum("tf,df->td", hidden, mlp_w[2], preferred_element_type=jnp.float32)
        return mlp_part.astype(jnp.bfloat16)

    attn_part0 = attention_piece(0)
    attn_part0, kv_cache = lax.optimization_barrier((attn_part0, kv_cache))
    mid0, rows0 = mid_of(0, attn_part0)
    attn_part1 = attention_piece(1)
    attn_part1, rows0 = lax.optimization_barrier((attn_part1, rows0))
    mid1, rows1 = mid_of(1, attn_part1)
    mlp_part0 = mlp_of(rows0)
    mlp_part0, rows1 = lax.optimization_barrier((mlp_part0, rows1))
    mlp_mine0 = sum_rows(mlp_part0, "tensor")
    mlp_mine1 = sum_rows(mlp_of(rows1), "tensor")
    outputs = [
        (mid0.astype(jnp.float32) + mlp_mine0).astype(jnp.bfloat16),
        (mid1.astype(jnp.float32) + mlp_mine1).astype(jnp.bfloat16),
    ]
    layer_out = jnp.concatenate(outputs, axis=0)
    return (layer_out, kv_cache)


def solution(mesh):
    return jax.shard_map(
        body,
        mesh=mesh,
        in_specs=(
            P(("dp", "tensor"), None),
            P("dp"),
            P("dp"),
            P(None, "dp", "tensor"),
            P("tensor", "dp"),
            P(None, "dp", "tensor"),
            P("tensor", "dp"),
            P("dp"),
        ),
        out_specs=(P(("dp", "tensor"), None), P("dp", None, None, "tensor")),
        check_vma=False,
    )
```

```python
import math

import jax
import jax.numpy as jnp
from jax import lax
from jax.sharding import PartitionSpec as P

HD = 128


def layer_norm(values):
    values = values.astype(jnp.float32)
    center = values - jnp.mean(values, axis=-1, keepdims=True)
    spread = jnp.mean(center * center, axis=-1, keepdims=True)
    return center * lax.rsqrt(spread + 1e-05)


def rotate(values, position):
    half = values.shape[-1] // 2
    freq = 10000.0 ** (-jnp.arange(half, dtype=jnp.float32) * 2.0 / values.shape[-1])
    angle = position.astype(jnp.float32)[:, None] * freq[None, :]
    cosine = jnp.cos(angle)[:, None, :]
    sine = jnp.sin(angle)[:, None, :]
    first = values[..., :half]
    second = values[..., half:]
    return jnp.concatenate(
        [first * cosine - second * sine, second * cosine + first * sine], axis=-1
    )


def row_folder(source, piece):
    return jnp.einsum("td,cdf->ctf", source, piece, preferred_element_type=jnp.float32)


def attend(query, keys, values, segment):
    tokens = query.shape[0]
    block = min(512, tokens)
    scale = 1.0 / math.sqrt(HD)
    order = jnp.arange(tokens)
    outputs = []
    for first in range(0, tokens, block):
        last = first + block
        scores = (
            jnp.einsum(
                "qhd,khd->hqk", query[first:last], keys[:last], preferred_element_type=jnp.float32
            )
            * scale
        )
        allowed = (segment[first:last, None] == segment[None, :last]) & (
            order[None, :last] <= order[first:last, None]
        )
        top = jnp.max(jnp.where(allowed[None], scores, -1e30), axis=-1, keepdims=True)
        weights = jnp.exp(jnp.where(allowed[None], scores - top, -1e30))
        total = jnp.sum(weights, axis=-1)
        mixed = jnp.einsum(
            "hqk,khd->qhd",
            weights.astype(jnp.bfloat16),
            values[:last],
            preferred_element_type=jnp.float32,
        )
        outputs.append((mixed / jnp.transpose(total)[:, :, None]).astype(jnp.bfloat16))
    return jnp.concatenate(outputs, axis=0).reshape(tokens, -1)


def write_cache(keys, values, page_table):
    tokens = keys.shape[0]
    width = keys.shape[1] * keys.shape[2]
    pages = page_table.shape[0]
    page_size = tokens // pages
    owners = lax.axis_size("dp")
    per_owner = pages // owners
    stacked = jnp.stack([keys.reshape(tokens, width), values.reshape(tokens, width)], axis=0)
    stacked = stacked.reshape(2, pages, page_size, width).transpose(1, 0, 2, 3)
    page_table, stacked = lax.optimization_barrier((page_table, stacked))
    order = jnp.argsort(page_table // pages, stable=True)
    outgoing = stacked[order].reshape(owners, per_owner, 2, page_size, width)
    outgoing_ids = page_table[order].reshape(owners, per_owner)
    arrived, arrived_ids = (
        lax.all_to_all(outgoing, "dp", split_axis=0, concat_axis=0, tiled=True),
        lax.all_to_all(outgoing_ids, "dp", split_axis=0, concat_axis=0, tiled=True),
    )
    local = (arrived_ids - lax.axis_index("dp") * pages).reshape(-1)
    empty = jnp.zeros((pages, 2, page_size, width), jnp.bfloat16)
    return empty.at[local].set(arrived.reshape(pages, 2, page_size, width))


def gather_packed(pieces, axis_name):
    rows = [piece.shape[0] for piece in pieces]
    packed = jnp.concatenate(pieces, axis=0)
    gathered = lax.all_gather(packed, axis_name, axis=0, tiled=False)
    outputs, first = [], 0
    for count in rows:
        outputs.append(gathered[:, first:first + count])
        first += count
    return outputs


def gather_rows(rows, axis_name):
    count = lax.axis_size(axis_name)
    copies = jnp.broadcast_to(rows[None], (count,) + rows.shape)
    gathered = lax.all_to_all(copies, axis_name, 0, 0, tiled=True)
    return gathered.reshape(count * rows.shape[0], rows.shape[1])


def sum_rows(terms, axis_name):
    count = lax.axis_size(axis_name)
    arrived = lax.all_to_all(
        terms.reshape(count, terms.shape[0] // count, terms.shape[1]), axis_name, 0, 0, tiled=True
    )
    return jnp.sum(arrived.astype(jnp.float32), axis=0)


def body(stream, segment, position, w_qkv, w_out, w_gate_up, w_down, page_table):
    tok_group = segment.shape[0]
    share_rows = stream.shape[0]
    local_cols = w_qkv.shape[2]
    attn_w = lax.all_gather(
        jnp.concatenate([w_qkv, jnp.transpose(w_out)[None]], axis=0), "dp", axis=1, tiled=True
    )
    mlp_w = lax.all_gather(
        jnp.concatenate([w_gate_up, jnp.transpose(w_down)[None]], axis=0), "dp", axis=1, tiled=True
    )
    full_stream = gather_rows(stream, "tensor")
    normed = layer_norm(full_stream).astype(jnp.bfloat16)
    local_heads = local_cols // HD
    projected = jnp.einsum("td,cdf->ctf", normed, attn_w[:3], preferred_element_type=jnp.float32)
    query = rotate(projected[0].reshape(tok_group, local_heads, HD), position).astype(jnp.bfloat16)
    keys = rotate(projected[1].reshape(tok_group, local_heads, HD), position).astype(jnp.bfloat16)
    values = projected[2].reshape(tok_group, local_heads, HD).astype(jnp.bfloat16)
    kv_cache = write_cache(keys, values, page_table)
    context = attend(query, keys, values, segment)
    attn_part = jnp.einsum("tr,dr->td", context, attn_w[3], preferred_element_type=jnp.float32)
    attn_part, kv_cache = lax.optimization_barrier((attn_part.astype(jnp.bfloat16), kv_cache))
    attn_mine = sum_rows(attn_part, "tensor")
    mid = (stream.astype(jnp.float32) + attn_mine).astype(jnp.bfloat16)
    normed2_mine = layer_norm(mid).astype(jnp.bfloat16)
    pieces = 2
    piece = share_rows // pieces
    mlp_pieces = []
    for first in range(0, share_rows, piece):
        rows = gather_rows(normed2_mine[first:first + piece], "tensor")
        gate_up = jnp.einsum("td,cdf->ctf", rows, mlp_w[:2], preferred_element_type=jnp.float32)
        hidden = (jax.nn.silu(gate_up[0]) * gate_up[1]).astype(jnp.bfloat16)
        mlp_part = jnp.einsum("tf,df->td", hidden, mlp_w[2], preferred_element_type=jnp.float32)
        mlp_pieces.append(sum_rows(mlp_part.astype(jnp.bfloat16), "tensor"))
    mlp_mine = jnp.concatenate(mlp_pieces, axis=0)
    layer_out = (mid.astype(jnp.float32) + mlp_mine).astype(jnp.bfloat16)
    return (layer_out, kv_cache)


def solution(mesh):
    return jax.shard_map(
        body,
        mesh=mesh,
        in_specs=(
            P(("dp", "tensor"), None),
            P("dp"),
            P("dp"),
            P(None, "dp", "tensor"),
            P("tensor", "dp"),
            P(None, "dp", "tensor"),
            P("tensor", "dp"),
            P("dp"),
        ),
        out_specs=(P(("dp", "tensor"), None), P("dp", None, None, "tensor")),
        check_vma=False,
    )
```

```python
import math

import jax
import jax.numpy as jnp
from jax import lax
from jax.sharding import PartitionSpec as P

HD = 128


def layer_norm(values):
    values = values.astype(jnp.float32)
    center = values - jnp.mean(values, axis=-1, keepdims=True)
    spread = jnp.mean(center * center, axis=-1, keepdims=True)
    return center * lax.rsqrt(spread + 1e-05)


def rotate(values, position):
    half = values.shape[-1] // 2
    freq = 10000.0 ** (-jnp.arange(half, dtype=jnp.float32) * 2.0 / values.shape[-1])
    angle = position.astype(jnp.float32)[:, None] * freq[None, :]
    cosine = jnp.cos(angle)[:, None, :]
    sine = jnp.sin(angle)[:, None, :]
    first = values[..., :half]
    second = values[..., half:]
    return jnp.concatenate(
        [first * cosine - second * sine, second * cosine + first * sine], axis=-1
    )


def row_folder(source, piece):
    return jnp.einsum("td,cdf->ctf", source, piece, preferred_element_type=jnp.float32)


def attend(query, keys, values, segment):
    tokens = query.shape[0]
    block = min(512, tokens)
    scale = 1.0 / math.sqrt(HD)
    order = jnp.arange(tokens)
    outputs = []
    for first in range(0, tokens, block):
        last = first + block
        scores = (
            jnp.einsum(
                "qhd,khd->hqk", query[first:last], keys[:last], preferred_element_type=jnp.float32
            )
            * scale
        )
        allowed = (segment[first:last, None] == segment[None, :last]) & (
            order[None, :last] <= order[first:last, None]
        )
        top = jnp.max(jnp.where(allowed[None], scores, -1e30), axis=-1, keepdims=True)
        weights = jnp.exp(jnp.where(allowed[None], scores - top, -1e30))
        total = jnp.sum(weights, axis=-1)
        mixed = jnp.einsum(
            "hqk,khd->qhd",
            weights.astype(jnp.bfloat16),
            values[:last],
            preferred_element_type=jnp.float32,
        )
        outputs.append((mixed / jnp.transpose(total)[:, :, None]).astype(jnp.bfloat16))
    return jnp.concatenate(outputs, axis=0).reshape(tokens, -1)


def write_cache(keys, values, page_table):
    tokens = keys.shape[0]
    width = keys.shape[1] * keys.shape[2]
    pages = page_table.shape[0]
    page_size = tokens // pages
    owners = lax.axis_size("dp")
    per_owner = pages // owners
    stacked = jnp.stack([keys.reshape(tokens, width), values.reshape(tokens, width)], axis=0)
    stacked = stacked.reshape(2, pages, page_size, width).transpose(1, 0, 2, 3)
    page_table, stacked = lax.optimization_barrier((page_table, stacked))
    order = jnp.argsort(page_table // pages, stable=True)
    outgoing = stacked[order].reshape(owners, per_owner, 2, page_size, width)
    outgoing_ids = page_table[order].reshape(owners, per_owner)
    arrived, arrived_ids = (
        lax.all_to_all(outgoing, "dp", split_axis=0, concat_axis=0, tiled=True),
        lax.all_to_all(outgoing_ids, "dp", split_axis=0, concat_axis=0, tiled=True),
    )
    local = (arrived_ids - lax.axis_index("dp") * pages).reshape(-1)
    empty = jnp.zeros((pages, 2, page_size, width), jnp.bfloat16)
    return empty.at[local].set(arrived.reshape(pages, 2, page_size, width))


def gather_packed(pieces, axis_name):
    rows = [piece.shape[0] for piece in pieces]
    packed = jnp.concatenate(pieces, axis=0)
    gathered = lax.all_gather(packed, axis_name, axis=0, tiled=False)
    outputs, first = [], 0
    for count in rows:
        outputs.append(gathered[:, first:first + count])
        first += count
    return outputs


def gather_rows(rows, axis_name):
    count = lax.axis_size(axis_name)
    copies = jnp.broadcast_to(rows[None], (count,) + rows.shape)
    gathered = lax.all_to_all(copies, axis_name, 0, 0, tiled=True)
    return gathered.reshape(count * rows.shape[0], rows.shape[1])


def sum_rows(terms, axis_name):
    count = lax.axis_size(axis_name)
    arrived = lax.all_to_all(
        terms.reshape(count, terms.shape[0] // count, terms.shape[1]), axis_name, 0, 0, tiled=True
    )
    return jnp.sum(arrived.astype(jnp.float32), axis=0)


def body(stream, segment, position, w_qkv, w_out, w_gate_up, w_down, page_table):
    tok_group = segment.shape[0]
    share_rows = stream.shape[0]
    local_cols = w_qkv.shape[2]
    attn_w = lax.all_gather(
        jnp.concatenate([w_qkv, jnp.transpose(w_out)[None]], axis=0), "dp", axis=1, tiled=True
    )
    mlp_w = lax.all_gather(
        jnp.concatenate([w_gate_up, jnp.transpose(w_down)[None]], axis=0), "dp", axis=1, tiled=True
    )
    full_stream = gather_rows(stream, "tensor")
    normed = layer_norm(full_stream).astype(jnp.bfloat16)
    local_heads = local_cols // HD
    projected = jnp.einsum("td,cdf->ctf", normed, attn_w[:3], preferred_element_type=jnp.float32)
    query = rotate(projected[0].reshape(tok_group, local_heads, HD), position).astype(jnp.bfloat16)
    keys = rotate(projected[1].reshape(tok_group, local_heads, HD), position).astype(jnp.bfloat16)
    values = projected[2].reshape(tok_group, local_heads, HD).astype(jnp.bfloat16)
    kv_cache = write_cache(keys, values, page_table)
    context = attend(query, keys, values, segment)
    attn_part = jnp.einsum("tr,dr->td", context, attn_w[3], preferred_element_type=jnp.float32)
    attn_part, kv_cache = lax.optimization_barrier((attn_part.astype(jnp.bfloat16), kv_cache))
    attn_mine = sum_rows(attn_part, "tensor")
    mid = (stream.astype(jnp.float32) + attn_mine).astype(jnp.bfloat16)
    normed2_mine = layer_norm(mid).astype(jnp.bfloat16)
    pieces = 4
    piece = share_rows // pieces
    mlp_pieces = []
    for first in range(0, share_rows, piece):
        rows = gather_rows(normed2_mine[first:first + piece], "tensor")
        gate_up = jnp.einsum("td,cdf->ctf", rows, mlp_w[:2], preferred_element_type=jnp.float32)
        hidden = (jax.nn.silu(gate_up[0]) * gate_up[1]).astype(jnp.bfloat16)
        mlp_part = jnp.einsum("tf,df->td", hidden, mlp_w[2], preferred_element_type=jnp.float32)
        mlp_pieces.append(sum_rows(mlp_part.astype(jnp.bfloat16), "tensor"))
    mlp_mine = jnp.concatenate(mlp_pieces, axis=0)
    layer_out = (mid.astype(jnp.float32) + mlp_mine).astype(jnp.bfloat16)
    return (layer_out, kv_cache)


def solution(mesh):
    return jax.shard_map(
        body,
        mesh=mesh,
        in_specs=(
            P(("dp", "tensor"), None),
            P("dp"),
            P("dp"),
            P(None, "dp", "tensor"),
            P("tensor", "dp"),
            P(None, "dp", "tensor"),
            P("tensor", "dp"),
            P("dp"),
        ),
        out_specs=(P(("dp", "tensor"), None), P("dp", None, None, "tensor")),
        check_vma=False,
    )
```

```python
import math

import jax
import jax.numpy as jnp
from jax import lax
from jax.sharding import PartitionSpec as P

HD = 128


def layer_norm(values):
    values = values.astype(jnp.float32)
    center = values - jnp.mean(values, axis=-1, keepdims=True)
    spread = jnp.mean(center * center, axis=-1, keepdims=True)
    return center * lax.rsqrt(spread + 1e-05)


def rotate(values, position):
    half = values.shape[-1] // 2
    freq = 10000.0 ** (-jnp.arange(half, dtype=jnp.float32) * 2.0 / values.shape[-1])
    angle = position.astype(jnp.float32)[:, None] * freq[None, :]
    cosine = jnp.cos(angle)[:, None, :]
    sine = jnp.sin(angle)[:, None, :]
    first = values[..., :half]
    second = values[..., half:]
    return jnp.concatenate(
        [first * cosine - second * sine, second * cosine + first * sine], axis=-1
    )


def row_folder(source, piece):
    return jnp.einsum("td,cdf->ctf", source, piece, preferred_element_type=jnp.float32)


def attend(query, keys, values, segment):
    tokens = query.shape[0]
    block = min(512, tokens)
    scale = 1.0 / math.sqrt(HD)
    order = jnp.arange(tokens)
    outputs = []
    for first in range(0, tokens, block):
        last = first + block
        scores = (
            jnp.einsum(
                "qhd,khd->hqk", query[first:last], keys[:last], preferred_element_type=jnp.float32
            )
            * scale
        )
        allowed = (segment[first:last, None] == segment[None, :last]) & (
            order[None, :last] <= order[first:last, None]
        )
        top = jnp.max(jnp.where(allowed[None], scores, -1e30), axis=-1, keepdims=True)
        weights = jnp.exp(jnp.where(allowed[None], scores - top, -1e30))
        total = jnp.sum(weights, axis=-1)
        mixed = jnp.einsum(
            "hqk,khd->qhd",
            weights.astype(jnp.bfloat16),
            values[:last],
            preferred_element_type=jnp.float32,
        )
        outputs.append((mixed / jnp.transpose(total)[:, :, None]).astype(jnp.bfloat16))
    return jnp.concatenate(outputs, axis=0).reshape(tokens, -1)


def write_cache(keys, values, page_table):
    tokens = keys.shape[0]
    width = keys.shape[1] * keys.shape[2]
    pages = page_table.shape[0]
    page_size = tokens // pages
    owners = lax.axis_size("dp")
    per_owner = pages // owners
    me = lax.axis_index("dp")
    stacked = jnp.stack([keys.reshape(tokens, width), values.reshape(tokens, width)], axis=0)
    stacked = stacked.reshape(2, pages, page_size, width).transpose(1, 0, 2, 3)
    page_table, stacked = lax.optimization_barrier((page_table, stacked))
    order = jnp.argsort(page_table // pages, stable=True)
    outgoing = stacked[order].reshape(owners, per_owner, 2, page_size, width)
    outgoing_ids = page_table[order].reshape(owners, per_owner)
    arrived = [lax.dynamic_index_in_dim(outgoing, me, 0, keepdims=False)]
    arrived_ids = [lax.dynamic_index_in_dim(outgoing_ids, me, 0, keepdims=False)]
    for shift in range(1, owners):
        target = (me + shift) % owners
        pairs = [(i, (i + shift) % owners) for i in range(owners)]
        arrived.append(
            lax.ppermute(lax.dynamic_index_in_dim(outgoing, target, 0, keepdims=False), "dp", pairs)
        )
        arrived_ids.append(
            lax.ppermute(lax.dynamic_index_in_dim(outgoing_ids, target, 0, keepdims=False), "dp", pairs)
        )
    local = (jnp.stack(arrived_ids) - me * pages).reshape(-1)
    empty = jnp.zeros((pages, 2, page_size, width), jnp.bfloat16)
    return empty.at[local].set(jnp.stack(arrived).reshape(pages, 2, page_size, width))


def gather_packed(pieces, axis_name):
    rows = [piece.shape[0] for piece in pieces]
    packed = jnp.concatenate(pieces, axis=0)
    gathered = lax.all_gather(packed, axis_name, axis=0, tiled=False)
    outputs, first = [], 0
    for count in rows:
        outputs.append(gathered[:, first:first + count])
        first += count
    return outputs


def gather_rows(rows, axis_name):
    count = lax.axis_size(axis_name)
    copies = jnp.broadcast_to(rows[None], (count,) + rows.shape)
    gathered = lax.all_to_all(copies, axis_name, 0, 0, tiled=True)
    return gathered.reshape(count * rows.shape[0], rows.shape[1])


def sum_rows(terms, axis_name):
    count = lax.axis_size(axis_name)
    arrived = lax.all_to_all(
        terms.reshape(count, terms.shape[0] // count, terms.shape[1]), axis_name, 0, 0, tiled=True
    )
    return jnp.sum(arrived.astype(jnp.float32), axis=0)


def body(stream, segment, position, w_qkv, w_out, w_gate_up, w_down, page_table):
    tok_group = segment.shape[0]
    share_rows = stream.shape[0]
    local_cols = w_qkv.shape[2]
    qkv_w = lax.all_gather(w_qkv, "dp", axis=1, tiled=True)
    out_w = lax.all_gather(jnp.transpose(w_out), "dp", axis=0, tiled=True)
    mlp_w = lax.all_gather(
        jnp.concatenate([w_gate_up, jnp.transpose(w_down)[None]], axis=0), "dp", axis=1, tiled=True
    )
    full_stream = gather_rows(stream, "tensor")
    normed = layer_norm(full_stream).astype(jnp.bfloat16)
    local_heads = local_cols // HD
    projected = jnp.einsum("td,cdf->ctf", normed, qkv_w, preferred_element_type=jnp.float32)
    query = rotate(projected[0].reshape(tok_group, local_heads, HD), position).astype(jnp.bfloat16)
    keys = rotate(projected[1].reshape(tok_group, local_heads, HD), position).astype(jnp.bfloat16)
    values = projected[2].reshape(tok_group, local_heads, HD).astype(jnp.bfloat16)
    kv_cache = write_cache(keys, values, page_table)
    context = attend(query, keys, values, segment)
    attn_part = jnp.einsum("tr,dr->td", context, out_w, preferred_element_type=jnp.float32)
    attn_part, kv_cache = lax.optimization_barrier((attn_part.astype(jnp.bfloat16), kv_cache))
    attn_mine = sum_rows(attn_part, "tensor")
    mid = (stream.astype(jnp.float32) + attn_mine).astype(jnp.bfloat16)
    normed2_mine = layer_norm(mid).astype(jnp.bfloat16)
    pieces = 2
    piece = share_rows // pieces
    mlp_pieces = []
    for first in range(0, share_rows, piece):
        rows = gather_rows(normed2_mine[first:first + piece], "tensor")
        gate_up = jnp.einsum("td,cdf->ctf", rows, mlp_w[:2], preferred_element_type=jnp.float32)
        hidden = (jax.nn.silu(gate_up[0]) * gate_up[1]).astype(jnp.bfloat16)
        mlp_part = jnp.einsum("tf,df->td", hidden, mlp_w[2], preferred_element_type=jnp.float32)
        mlp_pieces.append(sum_rows(mlp_part.astype(jnp.bfloat16), "tensor"))
    mlp_mine = jnp.concatenate(mlp_pieces, axis=0)
    layer_out = (mid.astype(jnp.float32) + mlp_mine).astype(jnp.bfloat16)
    return (layer_out, kv_cache)


def solution(mesh):
    return jax.shard_map(
        body,
        mesh=mesh,
        in_specs=(
            P(("dp", "tensor"), None),
            P("dp"),
            P("dp"),
            P(None, "dp", "tensor"),
            P("tensor", "dp"),
            P(None, "dp", "tensor"),
            P("tensor", "dp"),
            P("dp"),
        ),
        out_specs=(P(("dp", "tensor"), None), P("dp", None, None, "tensor")),
        check_vma=False,
    )
```

```python
import math

import numpy as np

import jax
import jax.numpy as jnp
from jax import lax
from jax.sharding import PartitionSpec as P

HD = 128


def layer_norm(values):
    values = values.astype(jnp.float32)
    center = values - jnp.mean(values, axis=-1, keepdims=True)
    spread = jnp.mean(center * center, axis=-1, keepdims=True)
    return center * lax.rsqrt(spread + 1e-05)


def rotate(values, position):
    half = values.shape[-1] // 2
    freq = 10000.0 ** (-jnp.arange(half, dtype=jnp.float32) * 2.0 / values.shape[-1])
    angle = position.astype(jnp.float32)[:, None] * freq[None, :]
    cosine = jnp.cos(angle)[:, None, :]
    sine = jnp.sin(angle)[:, None, :]
    first = values[..., :half]
    second = values[..., half:]
    return jnp.concatenate(
        [first * cosine - second * sine, second * cosine + first * sine], axis=-1
    )


def row_folder(source, piece):
    return jnp.einsum("td,cdf->ctf", source, piece, preferred_element_type=jnp.float32)


def attend(query, keys, values, segment):
    tokens = query.shape[0]
    block = min(512, tokens)
    scale = 1.0 / math.sqrt(HD)
    order = jnp.arange(tokens)
    outputs = []
    for first in range(0, tokens, block):
        last = first + block
        scores = (
            jnp.einsum(
                "qhd,khd->hqk", query[first:last], keys[:last], preferred_element_type=jnp.float32
            )
            * scale
        )
        allowed = (segment[first:last, None] == segment[None, :last]) & (
            order[None, :last] <= order[first:last, None]
        )
        top = jnp.max(jnp.where(allowed[None], scores, -1e30), axis=-1, keepdims=True)
        weights = jnp.exp(jnp.where(allowed[None], scores - top, -1e30))
        total = jnp.sum(weights, axis=-1)
        mixed = jnp.einsum(
            "hqk,khd->qhd",
            weights.astype(jnp.bfloat16),
            values[:last],
            preferred_element_type=jnp.float32,
        )
        outputs.append((mixed / jnp.transpose(total)[:, :, None]).astype(jnp.bfloat16))
    return jnp.concatenate(outputs, axis=0).reshape(tokens, -1)


def write_cache(keys, values, page_table):
    tokens = keys.shape[0]
    width = keys.shape[1] * keys.shape[2]
    pages = page_table.shape[0]
    page_size = tokens // pages
    owners = lax.axis_size("dp")
    per_owner = pages // owners
    me = lax.axis_index("dp")
    stacked = jnp.stack([keys.reshape(tokens, width), values.reshape(tokens, width)], axis=0)
    stacked = stacked.reshape(2, pages, page_size, width).transpose(1, 0, 2, 3)
    order = jnp.argsort(page_table // pages, stable=True)
    outgoing = stacked[order].reshape(owners, per_owner, 2, page_size, width)
    arrived = lax.all_to_all(outgoing, "dp", split_axis=0, concat_axis=0, tiled=True)
    every_table = lax.all_gather(page_table, "dp", axis=0, tiled=False)
    every_order = jnp.argsort(every_table // pages, axis=1, stable=True)
    every_sorted = jnp.take_along_axis(every_table, every_order, axis=1)
    arrived_ids = lax.dynamic_index_in_dim(
        every_sorted.reshape(owners, owners, per_owner), me, 1, keepdims=False
    )
    local = (arrived_ids - me * pages).reshape(-1)
    empty = jnp.zeros((pages, 2, page_size, width), jnp.bfloat16)
    return empty.at[local].set(arrived.reshape(pages, 2, page_size, width))


def gather_packed(pieces, axis_name):
    rows = [piece.shape[0] for piece in pieces]
    packed = jnp.concatenate(pieces, axis=0)
    gathered = lax.all_gather(packed, axis_name, axis=0, tiled=False)
    outputs, first = [], 0
    for count in rows:
        outputs.append(gathered[:, first:first + count])
        first += count
    return outputs


def gather_rows(rows, axis_name):
    count = lax.axis_size(axis_name)
    copies = jnp.broadcast_to(rows[None], (count,) + rows.shape)
    gathered = lax.all_to_all(copies, axis_name, 0, 0, tiled=True)
    return gathered.reshape(count * rows.shape[0], rows.shape[1])


def sum_rows(terms, axis_name):
    count = lax.axis_size(axis_name)
    arrived = lax.all_to_all(
        terms.reshape(count, terms.shape[0] // count, terms.shape[1]), axis_name, 0, 0, tiled=True
    )
    return jnp.sum(arrived.astype(jnp.float32), axis=0)


def attend_block(query, keys, values, seg_q, seg_k, q_index):
    scale = 1.0 / math.sqrt(HD)
    scores = (
        jnp.einsum("qhd,khd->hqk", query, keys, preferred_element_type=jnp.float32) * scale
    )
    allowed = (seg_q[:, None] == seg_k[None, :]) & (
        jnp.arange(keys.shape[0])[None, :] <= jnp.asarray(q_index)[:, None]
    )
    top = jnp.max(jnp.where(allowed[None], scores, -1e30), axis=-1, keepdims=True)
    weights = jnp.exp(jnp.where(allowed[None], scores - top, -1e30))
    total = jnp.sum(weights, axis=-1)
    mixed = jnp.einsum(
        "hqk,khd->qhd", weights.astype(jnp.bfloat16), values, preferred_element_type=jnp.float32
    )
    mixed = (mixed / jnp.transpose(total)[:, :, None]).astype(jnp.bfloat16)
    return mixed.reshape(query.shape[0], -1)


def body(stream, segment, position, w_qkv, w_out, w_gate_up, w_down, page_table):
    tok_group = segment.shape[0]
    share_rows = stream.shape[0]
    shares = tok_group // share_rows
    local_cols = w_qkv.shape[2]
    attn_w = lax.all_gather(
        jnp.concatenate([w_qkv, jnp.transpose(w_out)[None]], axis=0), "dp", axis=1, tiled=True
    )
    mlp_w = lax.all_gather(
        jnp.concatenate([w_gate_up, jnp.transpose(w_down)[None]], axis=0), "dp", axis=1, tiled=True
    )
    full_stream = gather_rows(stream, "tensor")
    normed = layer_norm(full_stream).astype(jnp.bfloat16)
    local_heads = local_cols // HD
    projected = jnp.einsum("td,cdf->ctf", normed, attn_w[:3], preferred_element_type=jnp.float32)
    query = rotate(projected[0].reshape(tok_group, local_heads, HD), position).astype(jnp.bfloat16)
    keys = rotate(projected[1].reshape(tok_group, local_heads, HD), position).astype(jnp.bfloat16)
    values = projected[2].reshape(tok_group, local_heads, HD).astype(jnp.bfloat16)
    kv_cache = write_cache(keys, values, page_table)

    pieces = 2
    piece = share_rows // pieces
    span = 2
    query_grid = query.reshape(shares, pieces, piece, local_heads, HD)
    segment_grid = segment.reshape(shares, pieces, piece)
    index_grid = np.arange(tok_group).reshape(shares, pieces, piece)

    def attention_piece(p):
        blocks = []
        for s in range(0, shares, span):
            k_len = (s + span) * share_rows
            blocks.append(
                attend_block(
                    query_grid[s:s + span, p].reshape(span * piece, local_heads, HD),
                    keys[:k_len],
                    values[:k_len],
                    segment_grid[s:s + span, p].reshape(span * piece),
                    segment[:k_len],
                    index_grid[s:s + span, p].reshape(span * piece),
                )
            )
        context = jnp.concatenate(blocks, axis=0)
        attn_part = jnp.einsum("tr,dr->td", context, attn_w[3], preferred_element_type=jnp.float32)
        return attn_part.astype(jnp.bfloat16)

    def mid_of(p, attn_part):
        attn_mine = sum_rows(attn_part, "tensor")
        mid = (stream[p * piece:(p + 1) * piece].astype(jnp.float32) + attn_mine).astype(
            jnp.bfloat16
        )
        return mid, gather_rows(layer_norm(mid).astype(jnp.bfloat16), "tensor")

    def mlp_of(rows):
        gate_up = jnp.einsum("td,cdf->ctf", rows, mlp_w[:2], preferred_element_type=jnp.float32)
        hidden = (jax.nn.silu(gate_up[0]) * gate_up[1]).astype(jnp.bfloat16)
        mlp_part = jnp.einsum("tf,df->td", hidden, mlp_w[2], preferred_element_type=jnp.float32)
        return mlp_part.astype(jnp.bfloat16)

    attn_part0 = attention_piece(0)
    attn_part0, kv_cache = lax.optimization_barrier((attn_part0, kv_cache))
    mid0, rows0 = mid_of(0, attn_part0)
    attn_part1 = attention_piece(1)
    attn_part1, rows0 = lax.optimization_barrier((attn_part1, rows0))
    mid1, rows1 = mid_of(1, attn_part1)
    mlp_part0 = mlp_of(rows0)
    mlp_part0, rows1 = lax.optimization_barrier((mlp_part0, rows1))
    mlp_mine0 = sum_rows(mlp_part0, "tensor")
    mlp_mine1 = sum_rows(mlp_of(rows1), "tensor")
    outputs = [
        (mid0.astype(jnp.float32) + mlp_mine0).astype(jnp.bfloat16),
        (mid1.astype(jnp.float32) + mlp_mine1).astype(jnp.bfloat16),
    ]
    layer_out = jnp.concatenate(outputs, axis=0)
    return (layer_out, kv_cache)


def solution(mesh):
    return jax.shard_map(
        body,
        mesh=mesh,
        in_specs=(
            P(("dp", "tensor"), None),
            P("dp"),
            P("dp"),
            P(None, "dp", "tensor"),
            P("tensor", "dp"),
            P(None, "dp", "tensor"),
            P("tensor", "dp"),
            P("dp"),
        ),
        out_specs=(P(("dp", "tensor"), None), P("dp", None, None, "tensor")),
        check_vma=False,
    )
```

```python
import math

import numpy as np

import jax
import jax.numpy as jnp
from jax import lax
from jax.sharding import PartitionSpec as P

HD = 128


def layer_norm(values):
    values = values.astype(jnp.float32)
    center = values - jnp.mean(values, axis=-1, keepdims=True)
    spread = jnp.mean(center * center, axis=-1, keepdims=True)
    return center * lax.rsqrt(spread + 1e-05)


def rotate(values, position):
    half = values.shape[-1] // 2
    freq = 10000.0 ** (-jnp.arange(half, dtype=jnp.float32) * 2.0 / values.shape[-1])
    angle = position.astype(jnp.float32)[:, None] * freq[None, :]
    cosine = jnp.cos(angle)[:, None, :]
    sine = jnp.sin(angle)[:, None, :]
    first = values[..., :half]
    second = values[..., half:]
    return jnp.concatenate(
        [first * cosine - second * sine, second * cosine + first * sine], axis=-1
    )


def row_folder(source, piece):
    return jnp.einsum("td,cdf->ctf", source, piece, preferred_element_type=jnp.float32)


def attend(query, keys, values, segment):
    tokens = query.shape[0]
    block = min(512, tokens)
    scale = 1.0 / math.sqrt(HD)
    order = jnp.arange(tokens)
    outputs = []
    for first in range(0, tokens, block):
        last = first + block
        scores = (
            jnp.einsum(
                "qhd,khd->hqk", query[first:last], keys[:last], preferred_element_type=jnp.float32
            )
            * scale
        )
        allowed = (segment[first:last, None] == segment[None, :last]) & (
            order[None, :last] <= order[first:last, None]
        )
        top = jnp.max(jnp.where(allowed[None], scores, -1e30), axis=-1, keepdims=True)
        weights = jnp.exp(jnp.where(allowed[None], scores - top, -1e30))
        total = jnp.sum(weights, axis=-1)
        mixed = jnp.einsum(
            "hqk,khd->qhd",
            weights.astype(jnp.bfloat16),
            values[:last],
            preferred_element_type=jnp.float32,
        )
        outputs.append((mixed / jnp.transpose(total)[:, :, None]).astype(jnp.bfloat16))
    return jnp.concatenate(outputs, axis=0).reshape(tokens, -1)


def write_cache(keys, values, page_table):
    tokens = keys.shape[0]
    width = keys.shape[1] * keys.shape[2]
    pages = page_table.shape[0]
    page_size = tokens // pages
    owners = lax.axis_size("dp")
    per_owner = pages // owners
    me = lax.axis_index("dp")
    base = 128
    stacked = jnp.stack([keys.reshape(tokens, width), values.reshape(tokens, width)], axis=0)
    stacked = stacked.reshape(2, pages, page_size, width).transpose(1, 0, 2, 3)
    order = jnp.argsort(page_table // pages, stable=True)
    sorted_ids = page_table[order].reshape(owners, per_owner)
    code = jnp.stack([sorted_ids // base, sorted_ids % base], axis=-1).astype(jnp.bfloat16)
    slab = jnp.zeros((owners, 1, 2, page_size, width), jnp.bfloat16)
    slab = slab.at[:, 0, 0, 0, : 2 * per_owner].set(code.reshape(owners, 2 * per_owner))
    outgoing = jnp.concatenate(
        [stacked[order].reshape(owners, per_owner, 2, page_size, width), slab], axis=1
    )
    arrived = lax.all_to_all(outgoing, "dp", split_axis=0, concat_axis=0, tiled=True)
    codes = arrived[:, per_owner, 0, 0, : 2 * per_owner].astype(jnp.int32)
    codes = codes.reshape(owners, per_owner, 2)
    local = (codes[..., 0] * base + codes[..., 1] - me * pages).reshape(-1)
    empty = jnp.zeros((pages, 2, page_size, width), jnp.bfloat16)
    return empty.at[local].set(arrived[:, :per_owner].reshape(pages, 2, page_size, width))


def gather_packed(pieces, axis_name):
    rows = [piece.shape[0] for piece in pieces]
    packed = jnp.concatenate(pieces, axis=0)
    gathered = lax.all_gather(packed, axis_name, axis=0, tiled=False)
    outputs, first = [], 0
    for count in rows:
        outputs.append(gathered[:, first:first + count])
        first += count
    return outputs


def gather_rows(rows, axis_name):
    count = lax.axis_size(axis_name)
    copies = jnp.broadcast_to(rows[None], (count,) + rows.shape)
    gathered = lax.all_to_all(copies, axis_name, 0, 0, tiled=True)
    return gathered.reshape(count * rows.shape[0], rows.shape[1])


def sum_rows(terms, axis_name):
    count = lax.axis_size(axis_name)
    arrived = lax.all_to_all(
        terms.reshape(count, terms.shape[0] // count, terms.shape[1]), axis_name, 0, 0, tiled=True
    )
    return jnp.sum(arrived.astype(jnp.float32), axis=0)


def attend_block(query, keys, values, seg_q, seg_k, q_index):
    scale = 1.0 / math.sqrt(HD)
    scores = (
        jnp.einsum("qhd,khd->hqk", query, keys, preferred_element_type=jnp.float32) * scale
    )
    allowed = (seg_q[:, None] == seg_k[None, :]) & (
        jnp.arange(keys.shape[0])[None, :] <= jnp.asarray(q_index)[:, None]
    )
    top = jnp.max(jnp.where(allowed[None], scores, -1e30), axis=-1, keepdims=True)
    weights = jnp.exp(jnp.where(allowed[None], scores - top, -1e30))
    total = jnp.sum(weights, axis=-1)
    mixed = jnp.einsum(
        "hqk,khd->qhd", weights.astype(jnp.bfloat16), values, preferred_element_type=jnp.float32
    )
    mixed = (mixed / jnp.transpose(total)[:, :, None]).astype(jnp.bfloat16)
    return mixed.reshape(query.shape[0], -1)


def body(stream, segment, position, w_qkv, w_out, w_gate_up, w_down, page_table):
    tok_group = segment.shape[0]
    share_rows = stream.shape[0]
    shares = tok_group // share_rows
    local_cols = w_qkv.shape[2]
    attn_w = lax.all_gather(
        jnp.concatenate([w_qkv, jnp.transpose(w_out)[None]], axis=0), "dp", axis=1, tiled=True
    )
    mlp_w = lax.all_gather(
        jnp.concatenate([w_gate_up, jnp.transpose(w_down)[None]], axis=0), "dp", axis=1, tiled=True
    )
    full_stream = gather_rows(stream, "tensor")
    normed = layer_norm(full_stream).astype(jnp.bfloat16)
    local_heads = local_cols // HD
    projected = jnp.einsum("td,cdf->ctf", normed, attn_w[:3], preferred_element_type=jnp.float32)
    query = rotate(projected[0].reshape(tok_group, local_heads, HD), position).astype(jnp.bfloat16)
    keys = rotate(projected[1].reshape(tok_group, local_heads, HD), position).astype(jnp.bfloat16)
    values = projected[2].reshape(tok_group, local_heads, HD).astype(jnp.bfloat16)
    kv_cache = write_cache(keys, values, page_table)

    pieces = 2
    piece = share_rows // pieces
    span = 2
    query_grid = query.reshape(shares, pieces, piece, local_heads, HD)
    segment_grid = segment.reshape(shares, pieces, piece)
    index_grid = np.arange(tok_group).reshape(shares, pieces, piece)

    def attention_piece(p):
        blocks = []
        for s in range(0, shares, span):
            k_len = (s + span) * share_rows
            blocks.append(
                attend_block(
                    query_grid[s:s + span, p].reshape(span * piece, local_heads, HD),
                    keys[:k_len],
                    values[:k_len],
                    segment_grid[s:s + span, p].reshape(span * piece),
                    segment[:k_len],
                    index_grid[s:s + span, p].reshape(span * piece),
                )
            )
        context = jnp.concatenate(blocks, axis=0)
        attn_part = jnp.einsum("tr,dr->td", context, attn_w[3], preferred_element_type=jnp.float32)
        return attn_part.astype(jnp.bfloat16)

    def mid_of(p, attn_part):
        attn_mine = sum_rows(attn_part, "tensor")
        mid = (stream[p * piece:(p + 1) * piece].astype(jnp.float32) + attn_mine).astype(
            jnp.bfloat16
        )
        return mid, gather_rows(layer_norm(mid).astype(jnp.bfloat16), "tensor")

    def mlp_of(rows):
        gate_up = jnp.einsum("td,cdf->ctf", rows, mlp_w[:2], preferred_element_type=jnp.float32)
        hidden = (jax.nn.silu(gate_up[0]) * gate_up[1]).astype(jnp.bfloat16)
        mlp_part = jnp.einsum("tf,df->td", hidden, mlp_w[2], preferred_element_type=jnp.float32)
        return mlp_part.astype(jnp.bfloat16)

    attn_part0 = attention_piece(0)
    attn_part0, kv_cache = lax.optimization_barrier((attn_part0, kv_cache))
    mid0, rows0 = mid_of(0, attn_part0)
    attn_part1 = attention_piece(1)
    attn_part1, rows0 = lax.optimization_barrier((attn_part1, rows0))
    mid1, rows1 = mid_of(1, attn_part1)
    mlp_part0 = mlp_of(rows0)
    mlp_part0, rows1 = lax.optimization_barrier((mlp_part0, rows1))
    mlp_mine0 = sum_rows(mlp_part0, "tensor")
    mlp_mine1 = sum_rows(mlp_of(rows1), "tensor")
    outputs = [
        (mid0.astype(jnp.float32) + mlp_mine0).astype(jnp.bfloat16),
        (mid1.astype(jnp.float32) + mlp_mine1).astype(jnp.bfloat16),
    ]
    layer_out = jnp.concatenate(outputs, axis=0)
    return (layer_out, kv_cache)


def solution(mesh):
    return jax.shard_map(
        body,
        mesh=mesh,
        in_specs=(
            P(("dp", "tensor"), None),
            P("dp"),
            P("dp"),
            P(None, "dp", "tensor"),
            P("tensor", "dp"),
            P(None, "dp", "tensor"),
            P("tensor", "dp"),
            P("dp"),
        ),
        out_specs=(P(("dp", "tensor"), None), P("dp", None, None, "tensor")),
        check_vma=False,
    )
```

```python
import math

import numpy as np

import jax
import jax.numpy as jnp
from jax import lax
from jax.sharding import PartitionSpec as P

HD = 128
DP = ("chips", "core")


def layer_norm(values):
    values = values.astype(jnp.float32)
    center = values - jnp.mean(values, axis=-1, keepdims=True)
    spread = jnp.mean(center * center, axis=-1, keepdims=True)
    return center * lax.rsqrt(spread + 1e-05)


def rotate(values, position):
    half = values.shape[-1] // 2
    freq = 10000.0 ** (-jnp.arange(half, dtype=jnp.float32) * 2.0 / values.shape[-1])
    angle = position.astype(jnp.float32)[:, None] * freq[None, :]
    cosine = jnp.cos(angle)[:, None, :]
    sine = jnp.sin(angle)[:, None, :]
    first = values[..., :half]
    second = values[..., half:]
    return jnp.concatenate(
        [first * cosine - second * sine, second * cosine + first * sine], axis=-1
    )


def row_folder(source, piece):
    return jnp.einsum("td,cdf->ctf", source, piece, preferred_element_type=jnp.float32)


def attend(query, keys, values, segment):
    tokens = query.shape[0]
    block = min(512, tokens)
    scale = 1.0 / math.sqrt(HD)
    order = jnp.arange(tokens)
    outputs = []
    for first in range(0, tokens, block):
        last = first + block
        scores = (
            jnp.einsum(
                "qhd,khd->hqk", query[first:last], keys[:last], preferred_element_type=jnp.float32
            )
            * scale
        )
        allowed = (segment[first:last, None] == segment[None, :last]) & (
            order[None, :last] <= order[first:last, None]
        )
        top = jnp.max(jnp.where(allowed[None], scores, -1e30), axis=-1, keepdims=True)
        weights = jnp.exp(jnp.where(allowed[None], scores - top, -1e30))
        total = jnp.sum(weights, axis=-1)
        mixed = jnp.einsum(
            "hqk,khd->qhd",
            weights.astype(jnp.bfloat16),
            values[:last],
            preferred_element_type=jnp.float32,
        )
        outputs.append((mixed / jnp.transpose(total)[:, :, None]).astype(jnp.bfloat16))
    return jnp.concatenate(outputs, axis=0).reshape(tokens, -1)


def write_cache(keys, values, page_table):
    tokens = keys.shape[0]
    width = keys.shape[1] * keys.shape[2]
    pages = page_table.shape[0]
    page_size = tokens // pages
    owners = lax.axis_size(DP)
    per_owner = pages // owners
    me = lax.axis_index(DP)
    base = 128
    stacked = jnp.stack([keys.reshape(tokens, width), values.reshape(tokens, width)], axis=0)
    stacked = stacked.reshape(2, pages, page_size, width).transpose(1, 0, 2, 3)
    order = jnp.argsort(page_table // pages, stable=True)
    sorted_ids = page_table[order].reshape(owners, per_owner)
    code = jnp.stack([sorted_ids // base, sorted_ids % base], axis=-1).astype(jnp.bfloat16)
    slab = jnp.zeros((owners, 1, 2, page_size, width), jnp.bfloat16)
    slab = slab.at[:, 0, 0, 0, : 2 * per_owner].set(code.reshape(owners, 2 * per_owner))
    outgoing = jnp.concatenate(
        [stacked[order].reshape(owners, per_owner, 2, page_size, width), slab], axis=1
    )
    arrived = lax.all_to_all(outgoing, DP, split_axis=0, concat_axis=0, tiled=True)
    codes = arrived[:, per_owner, 0, 0, : 2 * per_owner].astype(jnp.int32)
    codes = codes.reshape(owners, per_owner, 2)
    local = (codes[..., 0] * base + codes[..., 1] - me * pages).reshape(-1)
    empty = jnp.zeros((pages, 2, page_size, width), jnp.bfloat16)
    return empty.at[local].set(arrived[:, :per_owner].reshape(pages, 2, page_size, width))


def gather_weights(piece):
    mine = lax.all_gather(piece, "chips", axis=1, tiled=False)
    other = lax.ppermute(mine, "core", [(0, 1), (1, 0)])
    first = lax.axis_index("core") == 0
    both = jnp.stack([jnp.where(first, mine, other), jnp.where(first, other, mine)], axis=2)
    return both.reshape(piece.shape[0], -1, piece.shape[2])


def gather_packed(pieces, axis_name):
    rows = [piece.shape[0] for piece in pieces]
    packed = jnp.concatenate(pieces, axis=0)
    gathered = lax.all_gather(packed, axis_name, axis=0, tiled=False)
    outputs, first = [], 0
    for count in rows:
        outputs.append(gathered[:, first:first + count])
        first += count
    return outputs


def gather_rows(rows, axis_name):
    count = lax.axis_size(axis_name)
    copies = jnp.broadcast_to(rows[None], (count,) + rows.shape)
    gathered = lax.all_to_all(copies, axis_name, 0, 0, tiled=True)
    return gathered.reshape(count * rows.shape[0], rows.shape[1])


def sum_rows(terms, axis_name):
    count = lax.axis_size(axis_name)
    arrived = lax.all_to_all(
        terms.reshape(count, terms.shape[0] // count, terms.shape[1]), axis_name, 0, 0, tiled=True
    )
    return jnp.sum(arrived.astype(jnp.float32), axis=0)


def attend_block(query, keys, values, seg_q, seg_k, q_index):
    scale = 1.0 / math.sqrt(HD)
    scores = (
        jnp.einsum("qhd,khd->hqk", query, keys, preferred_element_type=jnp.float32) * scale
    )
    allowed = (seg_q[:, None] == seg_k[None, :]) & (
        jnp.arange(keys.shape[0])[None, :] <= jnp.asarray(q_index)[:, None]
    )
    top = jnp.max(jnp.where(allowed[None], scores, -1e30), axis=-1, keepdims=True)
    weights = jnp.exp(jnp.where(allowed[None], scores - top, -1e30))
    total = jnp.sum(weights, axis=-1)
    mixed = jnp.einsum(
        "hqk,khd->qhd", weights.astype(jnp.bfloat16), values, preferred_element_type=jnp.float32
    )
    mixed = (mixed / jnp.transpose(total)[:, :, None]).astype(jnp.bfloat16)
    return mixed.reshape(query.shape[0], -1)


def body(stream, segment, position, w_qkv, w_out, w_gate_up, w_down, page_table):
    tok_group = segment.shape[0]
    share_rows = stream.shape[0]
    shares = tok_group // share_rows
    local_cols = w_qkv.shape[2]
    attn_w = gather_weights(jnp.concatenate([w_qkv, jnp.transpose(w_out)[None]], axis=0))
    mlp_w = gather_weights(jnp.concatenate([w_gate_up, jnp.transpose(w_down)[None]], axis=0))
    full_stream = gather_rows(stream, "tensor")
    normed = layer_norm(full_stream).astype(jnp.bfloat16)
    local_heads = local_cols // HD
    projected = jnp.einsum("td,cdf->ctf", normed, attn_w[:3], preferred_element_type=jnp.float32)
    query = rotate(projected[0].reshape(tok_group, local_heads, HD), position).astype(jnp.bfloat16)
    keys = rotate(projected[1].reshape(tok_group, local_heads, HD), position).astype(jnp.bfloat16)
    values = projected[2].reshape(tok_group, local_heads, HD).astype(jnp.bfloat16)
    kv_cache = write_cache(keys, values, page_table)

    pieces = 2
    piece = share_rows // pieces
    span = 2
    query_grid = query.reshape(shares, pieces, piece, local_heads, HD)
    segment_grid = segment.reshape(shares, pieces, piece)
    index_grid = np.arange(tok_group).reshape(shares, pieces, piece)

    def attention_piece(p):
        blocks = []
        for s in range(0, shares, span):
            k_len = (s + span) * share_rows
            blocks.append(
                attend_block(
                    query_grid[s:s + span, p].reshape(span * piece, local_heads, HD),
                    keys[:k_len],
                    values[:k_len],
                    segment_grid[s:s + span, p].reshape(span * piece),
                    segment[:k_len],
                    index_grid[s:s + span, p].reshape(span * piece),
                )
            )
        context = jnp.concatenate(blocks, axis=0)
        attn_part = jnp.einsum("tr,dr->td", context, attn_w[3], preferred_element_type=jnp.float32)
        return attn_part.astype(jnp.bfloat16)

    def mid_of(p, attn_part):
        attn_mine = sum_rows(attn_part, "tensor")
        mid = (stream[p * piece:(p + 1) * piece].astype(jnp.float32) + attn_mine).astype(
            jnp.bfloat16
        )
        return mid, gather_rows(layer_norm(mid).astype(jnp.bfloat16), "tensor")

    def mlp_of(rows):
        gate_up = jnp.einsum("td,cdf->ctf", rows, mlp_w[:2], preferred_element_type=jnp.float32)
        hidden = (jax.nn.silu(gate_up[0]) * gate_up[1]).astype(jnp.bfloat16)
        mlp_part = jnp.einsum("tf,df->td", hidden, mlp_w[2], preferred_element_type=jnp.float32)
        return mlp_part.astype(jnp.bfloat16)

    attn_part0 = attention_piece(0)
    attn_part0, kv_cache = lax.optimization_barrier((attn_part0, kv_cache))
    mid0, rows0 = mid_of(0, attn_part0)
    attn_part1 = attention_piece(1)
    attn_part1, rows0 = lax.optimization_barrier((attn_part1, rows0))
    mid1, rows1 = mid_of(1, attn_part1)
    mlp_part0 = mlp_of(rows0)
    mlp_part0, rows1 = lax.optimization_barrier((mlp_part0, rows1))
    mlp_mine0 = sum_rows(mlp_part0, "tensor")
    mlp_mine1 = sum_rows(mlp_of(rows1), "tensor")
    outputs = [
        (mid0.astype(jnp.float32) + mlp_mine0).astype(jnp.bfloat16),
        (mid1.astype(jnp.float32) + mlp_mine1).astype(jnp.bfloat16),
    ]
    layer_out = jnp.concatenate(outputs, axis=0)
    return (layer_out, kv_cache)


def solution(mesh):
    dp_size = mesh.shape["dp"]
    split = jax.sharding.Mesh(
        mesh.devices.reshape(dp_size // 2, 2, mesh.shape["tensor"]), ("chips", "core", "tensor")
    )
    return jax.shard_map(
        body,
        mesh=split,
        in_specs=(
            P(DP + ("tensor",), None),
            P(DP),
            P(DP),
            P(None, DP, "tensor"),
            P("tensor", DP),
            P(None, DP, "tensor"),
            P("tensor", DP),
            P(DP),
        ),
        out_specs=(P(DP + ("tensor",), None), P(DP, None, None, "tensor")),
        check_vma=False,
    )
```

```python
import math

import jax
import jax.numpy as jnp
from jax import lax
from jax.sharding import PartitionSpec as P

HD = 128


def layer_norm(values):
    values = values.astype(jnp.float32)
    center = values - jnp.mean(values, axis=-1, keepdims=True)
    spread = jnp.mean(center * center, axis=-1, keepdims=True)
    return center * lax.rsqrt(spread + 1e-05)


def rotate(values, position):
    half = values.shape[-1] // 2
    freq = 10000.0 ** (-jnp.arange(half, dtype=jnp.float32) * 2.0 / values.shape[-1])
    angle = position.astype(jnp.float32)[:, None] * freq[None, :]
    cosine = jnp.cos(angle)[:, None, :]
    sine = jnp.sin(angle)[:, None, :]
    first = values[..., :half]
    second = values[..., half:]
    return jnp.concatenate(
        [first * cosine - second * sine, second * cosine + first * sine], axis=-1
    )


def row_folder(source, piece):
    return jnp.einsum("td,cdf->ctf", source, piece, preferred_element_type=jnp.float32)


def attend(query, keys, values, segment):
    tokens = query.shape[0]
    block = min(512, tokens)
    scale = 1.0 / math.sqrt(HD)
    order = jnp.arange(tokens)
    outputs = []
    for first in range(0, tokens, block):
        last = first + block
        scores = (
            jnp.einsum(
                "qhd,khd->hqk", query[first:last], keys[:last], preferred_element_type=jnp.float32
            )
            * scale
        )
        allowed = (segment[first:last, None] == segment[None, :last]) & (
            order[None, :last] <= order[first:last, None]
        )
        top = jnp.max(jnp.where(allowed[None], scores, -1e30), axis=-1, keepdims=True)
        weights = jnp.exp(jnp.where(allowed[None], scores - top, -1e30))
        total = jnp.sum(weights, axis=-1)
        mixed = jnp.einsum(
            "hqk,khd->qhd",
            weights.astype(jnp.bfloat16),
            values[:last],
            preferred_element_type=jnp.float32,
        )
        outputs.append((mixed / jnp.transpose(total)[:, :, None]).astype(jnp.bfloat16))
    return jnp.concatenate(outputs, axis=0).reshape(tokens, -1)


def write_cache(keys, values, page_table):
    tokens = keys.shape[0]
    width = keys.shape[1] * keys.shape[2]
    pages = page_table.shape[0]
    page_size = tokens // pages
    owners = lax.axis_size("dp")
    per_owner = pages // owners
    me = lax.axis_index("dp")
    base = 128
    stacked = jnp.stack([keys.reshape(tokens, width), values.reshape(tokens, width)], axis=0)
    stacked = stacked.reshape(2, pages, page_size, width).transpose(1, 0, 2, 3)
    page_table, stacked = lax.optimization_barrier((page_table, stacked))
    order = jnp.argsort(page_table // pages, stable=True)
    sorted_ids = page_table[order].reshape(owners, per_owner)
    code = jnp.stack([sorted_ids // base, sorted_ids % base], axis=-1).astype(jnp.bfloat16)
    slab = jnp.zeros((owners, 1, 2, page_size, width), jnp.bfloat16)
    slab = slab.at[:, 0, 0, 0, : 2 * per_owner].set(code.reshape(owners, 2 * per_owner))
    outgoing = jnp.concatenate(
        [stacked[order].reshape(owners, per_owner, 2, page_size, width), slab], axis=1
    )
    arrived = lax.all_to_all(outgoing, "dp", split_axis=0, concat_axis=0, tiled=True)
    codes = arrived[:, per_owner, 0, 0, : 2 * per_owner].astype(jnp.int32)
    codes = codes.reshape(owners, per_owner, 2)
    local = (codes[..., 0] * base + codes[..., 1] - me * pages).reshape(-1)
    empty = jnp.zeros((pages, 2, page_size, width), jnp.bfloat16)
    return empty.at[local].set(arrived[:, :per_owner].reshape(pages, 2, page_size, width))


def gather_packed(pieces, axis_name):
    rows = [piece.shape[0] for piece in pieces]
    packed = jnp.concatenate(pieces, axis=0)
    gathered = lax.all_gather(packed, axis_name, axis=0, tiled=False)
    outputs, first = [], 0
    for count in rows:
        outputs.append(gathered[:, first:first + count])
        first += count
    return outputs


def gather_rows(rows, axis_name):
    count = lax.axis_size(axis_name)
    copies = jnp.broadcast_to(rows[None], (count,) + rows.shape)
    gathered = lax.all_to_all(copies, axis_name, 0, 0, tiled=True)
    return gathered.reshape(count * rows.shape[0], rows.shape[1])


def sum_rows(terms, axis_name):
    count = lax.axis_size(axis_name)
    arrived = lax.all_to_all(
        terms.reshape(count, terms.shape[0] // count, terms.shape[1]), axis_name, 0, 0, tiled=True
    )
    return jnp.sum(arrived.astype(jnp.float32), axis=0)


def body(stream, segment, position, w_qkv, w_out, w_gate_up, w_down, page_table):
    tok_group = segment.shape[0]
    share_rows = stream.shape[0]
    local_cols = w_qkv.shape[2]
    attn_w = lax.all_gather(
        jnp.concatenate([w_qkv, jnp.transpose(w_out)[None]], axis=0), "dp", axis=1, tiled=True
    )
    mlp_w = lax.all_gather(
        jnp.concatenate([w_gate_up, jnp.transpose(w_down)[None]], axis=0), "dp", axis=1, tiled=True
    )
    full_stream = gather_rows(stream, "tensor")
    normed = layer_norm(full_stream).astype(jnp.bfloat16)
    local_heads = local_cols // HD
    projected = jnp.einsum("td,cdf->ctf", normed, attn_w[:3], preferred_element_type=jnp.float32)
    query = rotate(projected[0].reshape(tok_group, local_heads, HD), position).astype(jnp.bfloat16)
    keys = rotate(projected[1].reshape(tok_group, local_heads, HD), position).astype(jnp.bfloat16)
    values = projected[2].reshape(tok_group, local_heads, HD).astype(jnp.bfloat16)
    kv_cache = write_cache(keys, values, page_table)
    context = attend(query, keys, values, segment)
    attn_part = jnp.einsum("tr,dr->td", context, attn_w[3], preferred_element_type=jnp.float32)
    attn_part, kv_cache = lax.optimization_barrier((attn_part.astype(jnp.bfloat16), kv_cache))
    attn_mine = sum_rows(attn_part, "tensor")
    mid = (stream.astype(jnp.float32) + attn_mine).astype(jnp.bfloat16)
    normed2_mine = layer_norm(mid).astype(jnp.bfloat16)
    pieces = 2
    piece = share_rows // pieces
    mlp_pieces = []
    for first in range(0, share_rows, piece):
        rows = gather_rows(normed2_mine[first:first + piece], "tensor")
        gate_up = jnp.einsum("td,cdf->ctf", rows, mlp_w[:2], preferred_element_type=jnp.float32)
        hidden = (jax.nn.silu(gate_up[0]) * gate_up[1]).astype(jnp.bfloat16)
        mlp_part = jnp.einsum("tf,df->td", hidden, mlp_w[2], preferred_element_type=jnp.float32)
        mlp_pieces.append(sum_rows(mlp_part.astype(jnp.bfloat16), "tensor"))
    mlp_mine = jnp.concatenate(mlp_pieces, axis=0)
    layer_out = (mid.astype(jnp.float32) + mlp_mine).astype(jnp.bfloat16)
    return (layer_out, kv_cache)


def solution(mesh):
    return jax.shard_map(
        body,
        mesh=mesh,
        in_specs=(
            P(("dp", "tensor"), None),
            P("dp"),
            P("dp"),
            P(None, "dp", "tensor"),
            P("tensor", "dp"),
            P(None, "dp", "tensor"),
            P("tensor", "dp"),
            P("dp"),
        ),
        out_specs=(P(("dp", "tensor"), None), P("dp", None, None, "tensor")),
        check_vma=False,
    )
```

```python
import math

import jax
import jax.numpy as jnp
from jax import lax
from jax.sharding import PartitionSpec as P

HD = 128


def layer_norm(values):
    values = values.astype(jnp.float32)
    center = values - jnp.mean(values, axis=-1, keepdims=True)
    spread = jnp.mean(center * center, axis=-1, keepdims=True)
    return center * lax.rsqrt(spread + 1e-05)


def rotate(values, position):
    half = values.shape[-1] // 2
    freq = 10000.0 ** (-jnp.arange(half, dtype=jnp.float32) * 2.0 / values.shape[-1])
    angle = position.astype(jnp.float32)[:, None] * freq[None, :]
    cosine = jnp.cos(angle)[:, None, :]
    sine = jnp.sin(angle)[:, None, :]
    first = values[..., :half]
    second = values[..., half:]
    return jnp.concatenate(
        [first * cosine - second * sine, second * cosine + first * sine], axis=-1
    )


def row_folder(source, piece):
    return jnp.einsum("td,cdf->ctf", source, piece, preferred_element_type=jnp.float32)


def attend(query, keys, values, segment):
    tokens = query.shape[0]
    block = min(512, tokens)
    scale = 1.0 / math.sqrt(HD)
    order = jnp.arange(tokens)
    outputs = []
    for first in range(0, tokens, block):
        last = first + block
        scores = (
            jnp.einsum(
                "qhd,khd->hqk", query[first:last], keys[:last], preferred_element_type=jnp.float32
            )
            * scale
        )
        allowed = (segment[first:last, None] == segment[None, :last]) & (
            order[None, :last] <= order[first:last, None]
        )
        top = jnp.max(jnp.where(allowed[None], scores, -1e30), axis=-1, keepdims=True)
        weights = jnp.exp(jnp.where(allowed[None], scores - top, -1e30))
        total = jnp.sum(weights, axis=-1)
        mixed = jnp.einsum(
            "hqk,khd->qhd",
            weights.astype(jnp.bfloat16),
            values[:last],
            preferred_element_type=jnp.float32,
        )
        outputs.append((mixed / jnp.transpose(total)[:, :, None]).astype(jnp.bfloat16))
    return jnp.concatenate(outputs, axis=0).reshape(tokens, -1)


def write_cache(keys, values, page_table):
    tokens = keys.shape[0]
    width = keys.shape[1] * keys.shape[2]
    pages = page_table.shape[0]
    page_size = tokens // pages
    owners = lax.axis_size("dp")
    per_owner = pages // owners
    me = lax.axis_index("dp")
    base = 128
    stacked = jnp.stack([keys.reshape(tokens, width), values.reshape(tokens, width)], axis=0)
    stacked = stacked.reshape(2, pages, page_size, width).transpose(1, 0, 2, 3)
    order = jnp.argsort(page_table // pages, stable=True)
    sorted_ids = page_table[order].reshape(owners, per_owner)
    code = jnp.stack([sorted_ids // base, sorted_ids % base], axis=-1).astype(jnp.bfloat16)
    slab = jnp.zeros((owners, 1, 2, page_size, width), jnp.bfloat16)
    slab = slab.at[:, 0, 0, 0, : 2 * per_owner].set(code.reshape(owners, 2 * per_owner))
    outgoing = jnp.concatenate(
        [stacked[order].reshape(owners, per_owner, 2, page_size, width), slab], axis=1
    )
    arrived = lax.all_to_all(outgoing, "dp", split_axis=0, concat_axis=0, tiled=True)
    codes = arrived[:, per_owner, 0, 0, : 2 * per_owner].astype(jnp.int32)
    codes = codes.reshape(owners, per_owner, 2)
    local = (codes[..., 0] * base + codes[..., 1] - me * pages).reshape(-1)
    empty = jnp.zeros((pages, 2, page_size, width), jnp.bfloat16)
    return empty.at[local].set(arrived[:, :per_owner].reshape(pages, 2, page_size, width))


def gather_packed(pieces, axis_name):
    rows = [piece.shape[0] for piece in pieces]
    packed = jnp.concatenate(pieces, axis=0)
    gathered = lax.all_gather(packed, axis_name, axis=0, tiled=False)
    outputs, first = [], 0
    for count in rows:
        outputs.append(gathered[:, first:first + count])
        first += count
    return outputs


def gather_rows(rows, axis_name):
    count = lax.axis_size(axis_name)
    copies = jnp.broadcast_to(rows[None], (count,) + rows.shape)
    gathered = lax.all_to_all(copies, axis_name, 0, 0, tiled=True)
    return gathered.reshape(count * rows.shape[0], rows.shape[1])


def sum_rows(terms, axis_name):
    count = lax.axis_size(axis_name)
    arrived = lax.all_to_all(
        terms.reshape(count, terms.shape[0] // count, terms.shape[1]), axis_name, 0, 0, tiled=True
    )
    return jnp.sum(arrived.astype(jnp.float32), axis=0)


def body(stream, segment, position, w_qkv, w_out, w_gate_up, w_down, page_table):
    tok_group = segment.shape[0]
    share_rows = stream.shape[0]
    local_cols = w_qkv.shape[2]
    attn_w = lax.all_gather(
        jnp.concatenate([w_qkv, jnp.transpose(w_out)[None]], axis=0), "dp", axis=1, tiled=True
    )
    mlp_w = lax.all_gather(
        jnp.concatenate([w_gate_up, jnp.transpose(w_down)[None]], axis=0), "dp", axis=1, tiled=True
    )
    normed = gather_rows(layer_norm(stream).astype(jnp.bfloat16), "tensor")
    local_heads = local_cols // HD
    projected = jnp.einsum("td,cdf->ctf", normed, attn_w[:3], preferred_element_type=jnp.float32)
    query = rotate(projected[0].reshape(tok_group, local_heads, HD), position).astype(jnp.bfloat16)
    keys = rotate(projected[1].reshape(tok_group, local_heads, HD), position).astype(jnp.bfloat16)
    values = projected[2].reshape(tok_group, local_heads, HD).astype(jnp.bfloat16)
    kv_cache = write_cache(keys, values, page_table)
    context = attend(query, keys, values, segment)
    attn_part = jnp.einsum("tr,dr->td", context, attn_w[3], preferred_element_type=jnp.float32)
    attn_part, kv_cache = lax.optimization_barrier((attn_part.astype(jnp.bfloat16), kv_cache))
    attn_mine = sum_rows(attn_part, "tensor")
    mid = (stream.astype(jnp.float32) + attn_mine).astype(jnp.bfloat16)
    normed2_mine = layer_norm(mid).astype(jnp.bfloat16)
    pieces = 2
    piece = share_rows // pieces
    mlp_pieces = []
    for first in range(0, share_rows, piece):
        rows = gather_rows(normed2_mine[first:first + piece], "tensor")
        gate_up = jnp.einsum("td,cdf->ctf", rows, mlp_w[:2], preferred_element_type=jnp.float32)
        hidden = (jax.nn.silu(gate_up[0]) * gate_up[1]).astype(jnp.bfloat16)
        mlp_part = jnp.einsum("tf,df->td", hidden, mlp_w[2], preferred_element_type=jnp.float32)
        mlp_pieces.append(sum_rows(mlp_part.astype(jnp.bfloat16), "tensor"))
    mlp_mine = jnp.concatenate(mlp_pieces, axis=0)
    layer_out = (mid.astype(jnp.float32) + mlp_mine).astype(jnp.bfloat16)
    return (layer_out, kv_cache)


def solution(mesh):
    return jax.shard_map(
        body,
        mesh=mesh,
        in_specs=(
            P(("dp", "tensor"), None),
            P("dp"),
            P("dp"),
            P(None, "dp", "tensor"),
            P("tensor", "dp"),
            P(None, "dp", "tensor"),
            P("tensor", "dp"),
            P("dp"),
        ),
        out_specs=(P(("dp", "tensor"), None), P("dp", None, None, "tensor")),
        check_vma=False,
    )
```

```python
import math

import jax
import jax.numpy as jnp
from jax import lax
from jax.sharding import PartitionSpec as P

HD = 128


def layer_norm(values):
    values = values.astype(jnp.float32)
    center = values - jnp.mean(values, axis=-1, keepdims=True)
    spread = jnp.mean(center * center, axis=-1, keepdims=True)
    return center * lax.rsqrt(spread + 1e-05)


def rotate(values, position):
    half = values.shape[-1] // 2
    freq = 10000.0 ** (-jnp.arange(half, dtype=jnp.float32) * 2.0 / values.shape[-1])
    angle = position.astype(jnp.float32)[:, None] * freq[None, :]
    cosine = jnp.cos(angle)[:, None, :]
    sine = jnp.sin(angle)[:, None, :]
    first = values[..., :half]
    second = values[..., half:]
    return jnp.concatenate(
        [first * cosine - second * sine, second * cosine + first * sine], axis=-1
    )


def row_folder(source, piece):
    return jnp.einsum("td,cdf->ctf", source, piece, preferred_element_type=jnp.float32)


def attend(query, keys, values, segment):
    tokens = query.shape[0]
    block = min(512, tokens)
    scale = 1.0 / math.sqrt(HD)
    order = jnp.arange(tokens)
    outputs = []
    for first in range(0, tokens, block):
        last = first + block
        scores = (
            jnp.einsum(
                "qhd,khd->hqk", query[first:last], keys[:last], preferred_element_type=jnp.float32
            )
            * scale
        )
        allowed = (segment[first:last, None] == segment[None, :last]) & (
            order[None, :last] <= order[first:last, None]
        )
        top = jnp.max(jnp.where(allowed[None], scores, -1e30), axis=-1, keepdims=True)
        weights = jnp.exp(jnp.where(allowed[None], scores - top, -1e30))
        total = jnp.sum(weights, axis=-1)
        mixed = jnp.einsum(
            "hqk,khd->qhd",
            weights.astype(jnp.bfloat16),
            values[:last],
            preferred_element_type=jnp.float32,
        )
        outputs.append((mixed / jnp.transpose(total)[:, :, None]).astype(jnp.bfloat16))
    return jnp.concatenate(outputs, axis=0).reshape(tokens, -1)


def write_cache(keys, values, page_table):
    tokens = keys.shape[0]
    width = keys.shape[1] * keys.shape[2]
    pages = page_table.shape[0]
    page_size = tokens // pages
    owners = lax.axis_size("dp")
    per_owner = pages // owners
    me = lax.axis_index("dp")
    base = 128
    stacked = jnp.stack([keys.reshape(tokens, width), values.reshape(tokens, width)], axis=0)
    stacked = stacked.reshape(2, pages, page_size, width).transpose(1, 0, 2, 3)
    page_table, stacked = lax.optimization_barrier((page_table, stacked))
    order = jnp.argsort(page_table // pages, stable=True)
    sorted_ids = page_table[order].reshape(owners, per_owner)
    code = jnp.stack([sorted_ids // base, sorted_ids % base], axis=-1).astype(jnp.bfloat16)
    slab = jnp.zeros((owners, 1, 2, page_size, width), jnp.bfloat16)
    slab = slab.at[:, 0, 0, 0, : 2 * per_owner].set(code.reshape(owners, 2 * per_owner))
    outgoing = jnp.concatenate(
        [stacked[order].reshape(owners, per_owner, 2, page_size, width), slab], axis=1
    )
    arrived = lax.all_to_all(outgoing, "dp", split_axis=0, concat_axis=0, tiled=True)
    codes = arrived[:, per_owner, 0, 0, : 2 * per_owner].astype(jnp.int32)
    codes = codes.reshape(owners, per_owner, 2)
    local = (codes[..., 0] * base + codes[..., 1] - me * pages).reshape(-1)
    empty = jnp.zeros((pages, 2, page_size, width), jnp.bfloat16)
    return empty.at[local].set(arrived[:, :per_owner].reshape(pages, 2, page_size, width))


def gather_packed(pieces, axis_name):
    rows = [piece.shape[0] for piece in pieces]
    packed = jnp.concatenate(pieces, axis=0)
    gathered = lax.all_gather(packed, axis_name, axis=0, tiled=False)
    outputs, first = [], 0
    for count in rows:
        outputs.append(gathered[:, first:first + count])
        first += count
    return outputs


def gather_rows(rows, axis_name):
    count = lax.axis_size(axis_name)
    copies = jnp.broadcast_to(rows[None], (count,) + rows.shape)
    gathered = lax.all_to_all(copies, axis_name, 0, 0, tiled=True)
    return gathered.reshape(count * rows.shape[0], rows.shape[1])


def sum_rows(terms, axis_name):
    count = lax.axis_size(axis_name)
    arrived = lax.all_to_all(
        terms.reshape(count, terms.shape[0] // count, terms.shape[1]), axis_name, 0, 0, tiled=True
    )
    return jnp.sum(arrived.astype(jnp.float32), axis=0)


def body(stream, segment, position, w_qkv, w_out, w_gate_up, w_down, page_table):
    tok_group = segment.shape[0]
    share_rows = stream.shape[0]
    local_cols = w_qkv.shape[2]
    attn_local = jnp.concatenate([w_qkv, jnp.transpose(w_out)[None]], axis=0)
    owners = lax.axis_size("dp")
    attn_w = lax.all_to_all(
        jnp.broadcast_to(attn_local[None], (owners,) + attn_local.shape), "dp", 0, 0, tiled=True
    )
    mlp_w = lax.all_gather(
        jnp.concatenate([w_gate_up, jnp.transpose(w_down)[None]], axis=0), "dp", axis=1, tiled=True
    )
    full_stream = lax.all_gather(stream, "tensor", axis=0, tiled=True)
    normed = layer_norm(full_stream).astype(jnp.bfloat16)
    normed = normed.reshape(tok_group, owners, normed.shape[1] // owners)
    local_heads = local_cols // HD
    projected = jnp.einsum("tgd,gcdf->ctf", normed, attn_w[:, :3], preferred_element_type=jnp.float32)
    query = rotate(projected[0].reshape(tok_group, local_heads, HD), position).astype(jnp.bfloat16)
    keys = rotate(projected[1].reshape(tok_group, local_heads, HD), position).astype(jnp.bfloat16)
    values = projected[2].reshape(tok_group, local_heads, HD).astype(jnp.bfloat16)
    kv_cache = write_cache(keys, values, page_table)
    context = attend(query, keys, values, segment)
    attn_part = jnp.einsum(
        "tr,gdr->tgd", context, attn_w[:, 3], preferred_element_type=jnp.float32
    ).reshape(tok_group, -1)
    attn_part, kv_cache = lax.optimization_barrier((attn_part.astype(jnp.bfloat16), kv_cache))
    attn_mine = sum_rows(attn_part, "tensor")
    mid = (stream.astype(jnp.float32) + attn_mine).astype(jnp.bfloat16)
    normed2_mine = layer_norm(mid).astype(jnp.bfloat16)
    pieces = 2
    piece = share_rows // pieces
    mlp_pieces = []
    for first in range(0, share_rows, piece):
        rows = gather_rows(normed2_mine[first:first + piece], "tensor")
        gate_up = jnp.einsum("td,cdf->ctf", rows, mlp_w[:2], preferred_element_type=jnp.float32)
        hidden = (jax.nn.silu(gate_up[0]) * gate_up[1]).astype(jnp.bfloat16)
        mlp_part = jnp.einsum("tf,df->td", hidden, mlp_w[2], preferred_element_type=jnp.float32)
        mlp_pieces.append(sum_rows(mlp_part.astype(jnp.bfloat16), "tensor"))
    mlp_mine = jnp.concatenate(mlp_pieces, axis=0)
    layer_out = (mid.astype(jnp.float32) + mlp_mine).astype(jnp.bfloat16)
    return (layer_out, kv_cache)


def solution(mesh):
    return jax.shard_map(
        body,
        mesh=mesh,
        in_specs=(
            P(("dp", "tensor"), None),
            P("dp"),
            P("dp"),
            P(None, "dp", "tensor"),
            P("tensor", "dp"),
            P(None, "dp", "tensor"),
            P("tensor", "dp"),
            P("dp"),
        ),
        out_specs=(P(("dp", "tensor"), None), P("dp", None, None, "tensor")),
        check_vma=False,
    )
```

```python
import math

import jax
import jax.numpy as jnp
from jax import lax
from jax.sharding import PartitionSpec as P

HD = 128


def layer_norm(values):
    values = values.astype(jnp.float32)
    center = values - jnp.mean(values, axis=-1, keepdims=True)
    spread = jnp.mean(center * center, axis=-1, keepdims=True)
    return center * lax.rsqrt(spread + 1e-05)


def rotate(values, position):
    half = values.shape[-1] // 2
    freq = 10000.0 ** (-jnp.arange(half, dtype=jnp.float32) * 2.0 / values.shape[-1])
    angle = position.astype(jnp.float32)[:, None] * freq[None, :]
    cosine = jnp.cos(angle)[:, None, :]
    sine = jnp.sin(angle)[:, None, :]
    first = values[..., :half]
    second = values[..., half:]
    return jnp.concatenate(
        [first * cosine - second * sine, second * cosine + first * sine], axis=-1
    )


def row_folder(source, piece):
    return jnp.einsum("td,cdf->ctf", source, piece, preferred_element_type=jnp.float32)


def attend(query, keys, values, segment):
    tokens = query.shape[0]
    block = min(512, tokens)
    scale = 1.0 / math.sqrt(HD)
    order = jnp.arange(tokens)
    outputs = []
    for first in range(0, tokens, block):
        last = first + block
        scores = (
            jnp.einsum(
                "qhd,khd->hqk", query[first:last], keys[:last], preferred_element_type=jnp.float32
            )
            * scale
        )
        allowed = (segment[first:last, None] == segment[None, :last]) & (
            order[None, :last] <= order[first:last, None]
        )
        top = jnp.max(jnp.where(allowed[None], scores, -1e30), axis=-1, keepdims=True)
        weights = jnp.exp(jnp.where(allowed[None], scores - top, -1e30))
        total = jnp.sum(weights, axis=-1)
        mixed = jnp.einsum(
            "hqk,khd->qhd",
            weights.astype(jnp.bfloat16),
            values[:last],
            preferred_element_type=jnp.float32,
        )
        outputs.append((mixed / jnp.transpose(total)[:, :, None]).astype(jnp.bfloat16))
    return jnp.concatenate(outputs, axis=0).reshape(tokens, -1)


def write_cache(keys, values, page_table):
    tokens = keys.shape[0]
    width = keys.shape[1] * keys.shape[2]
    pages = page_table.shape[0]
    page_size = tokens // pages
    owners = lax.axis_size("dp")
    per_owner = pages // owners
    me = lax.axis_index("dp")
    base = 128
    stacked = jnp.stack([keys.reshape(tokens, width), values.reshape(tokens, width)], axis=0)
    stacked = stacked.reshape(2, pages, page_size, width).transpose(1, 0, 2, 3)
    page_table, stacked = lax.optimization_barrier((page_table, stacked))
    order = jnp.argsort(page_table // pages, stable=True)
    sorted_ids = page_table[order].reshape(owners, per_owner)
    code = jnp.stack([sorted_ids // base, sorted_ids % base], axis=-1).astype(jnp.bfloat16)
    slab = jnp.zeros((owners, 1, 2, page_size, width), jnp.bfloat16)
    slab = slab.at[:, 0, 0, 0, : 2 * per_owner].set(code.reshape(owners, 2 * per_owner))
    outgoing = jnp.concatenate(
        [stacked[order].reshape(owners, per_owner, 2, page_size, width), slab], axis=1
    )
    arrived = lax.all_to_all(outgoing, "dp", split_axis=0, concat_axis=0, tiled=True)
    codes = arrived[:, per_owner, 0, 0, : 2 * per_owner].astype(jnp.int32)
    codes = codes.reshape(owners, per_owner, 2)
    local = (codes[..., 0] * base + codes[..., 1] - me * pages).reshape(-1)
    empty = jnp.zeros((pages, 2, page_size, width), jnp.bfloat16)
    return empty.at[local].set(arrived[:, :per_owner].reshape(pages, 2, page_size, width))


def gather_packed(pieces, axis_name):
    rows = [piece.shape[0] for piece in pieces]
    packed = jnp.concatenate(pieces, axis=0)
    gathered = lax.all_gather(packed, axis_name, axis=0, tiled=False)
    outputs, first = [], 0
    for count in rows:
        outputs.append(gathered[:, first:first + count])
        first += count
    return outputs


def gather_rows(rows, axis_name):
    count = lax.axis_size(axis_name)
    copies = jnp.broadcast_to(rows[None], (count,) + rows.shape)
    gathered = lax.all_to_all(copies, axis_name, 0, 0, tiled=True)
    return gathered.reshape(count * rows.shape[0], rows.shape[1])


def sum_rows(terms, axis_name):
    count = lax.axis_size(axis_name)
    arrived = lax.all_to_all(
        terms.reshape(count, terms.shape[0] // count, terms.shape[1]), axis_name, 0, 0, tiled=True
    )
    return jnp.sum(arrived.astype(jnp.float32), axis=0)


def body(stream, segment, position, w_qkv, w_out, w_gate_up, w_down, page_table):
    tok_group = segment.shape[0]
    share_rows = stream.shape[0]
    local_cols = w_qkv.shape[2]
    qkv_w = lax.all_gather(w_qkv, "dp", axis=1, tiled=True)
    out_local = jnp.transpose(w_out)
    owners = lax.axis_size("dp")
    out_w = lax.all_to_all(
        jnp.broadcast_to(out_local[None], (owners,) + out_local.shape), "dp", 0, 0, tiled=True
    ).reshape(owners * out_local.shape[0], out_local.shape[1])
    mlp_w = lax.all_gather(
        jnp.concatenate([w_gate_up, jnp.transpose(w_down)[None]], axis=0), "dp", axis=1, tiled=True
    )
    full_stream = gather_rows(stream, "tensor")
    normed = layer_norm(full_stream).astype(jnp.bfloat16)
    local_heads = local_cols // HD
    projected = jnp.einsum("td,cdf->ctf", normed, qkv_w, preferred_element_type=jnp.float32)
    query = rotate(projected[0].reshape(tok_group, local_heads, HD), position).astype(jnp.bfloat16)
    keys = rotate(projected[1].reshape(tok_group, local_heads, HD), position).astype(jnp.bfloat16)
    values = projected[2].reshape(tok_group, local_heads, HD).astype(jnp.bfloat16)
    kv_cache = write_cache(keys, values, page_table)
    context = attend(query, keys, values, segment)
    attn_part = jnp.einsum("tr,dr->td", context, out_w, preferred_element_type=jnp.float32)
    attn_part, kv_cache = lax.optimization_barrier((attn_part.astype(jnp.bfloat16), kv_cache))
    attn_mine = sum_rows(attn_part, "tensor")
    mid = (stream.astype(jnp.float32) + attn_mine).astype(jnp.bfloat16)
    normed2_mine = layer_norm(mid).astype(jnp.bfloat16)
    pieces = 2
    piece = share_rows // pieces
    mlp_pieces = []
    for first in range(0, share_rows, piece):
        rows = gather_rows(normed2_mine[first:first + piece], "tensor")
        gate_up = jnp.einsum("td,cdf->ctf", rows, mlp_w[:2], preferred_element_type=jnp.float32)
        hidden = (jax.nn.silu(gate_up[0]) * gate_up[1]).astype(jnp.bfloat16)
        mlp_part = jnp.einsum("tf,df->td", hidden, mlp_w[2], preferred_element_type=jnp.float32)
        mlp_pieces.append(sum_rows(mlp_part.astype(jnp.bfloat16), "tensor"))
    mlp_mine = jnp.concatenate(mlp_pieces, axis=0)
    layer_out = (mid.astype(jnp.float32) + mlp_mine).astype(jnp.bfloat16)
    return (layer_out, kv_cache)


def solution(mesh):
    return jax.shard_map(
        body,
        mesh=mesh,
        in_specs=(
            P(("dp", "tensor"), None),
            P("dp"),
            P("dp"),
            P(None, "dp", "tensor"),
            P("tensor", "dp"),
            P(None, "dp", "tensor"),
            P("tensor", "dp"),
            P("dp"),
        ),
        out_specs=(P(("dp", "tensor"), None), P("dp", None, None, "tensor")),
        check_vma=False,
    )
```

```python
import math

import jax
import jax.numpy as jnp
from jax import lax
from jax.sharding import PartitionSpec as P

HD = 128


def layer_norm(values):
    values = values.astype(jnp.float32)
    center = values - jnp.mean(values, axis=-1, keepdims=True)
    spread = jnp.mean(center * center, axis=-1, keepdims=True)
    return center * lax.rsqrt(spread + 1e-05)


def rotate(values, position):
    half = values.shape[-1] // 2
    freq = 10000.0 ** (-jnp.arange(half, dtype=jnp.float32) * 2.0 / values.shape[-1])
    angle = position.astype(jnp.float32)[:, None] * freq[None, :]
    cosine = jnp.cos(angle)[:, None, :]
    sine = jnp.sin(angle)[:, None, :]
    first = values[..., :half]
    second = values[..., half:]
    return jnp.concatenate(
        [first * cosine - second * sine, second * cosine + first * sine], axis=-1
    )


def row_folder(source, piece):
    return jnp.einsum("td,cdf->ctf", source, piece, preferred_element_type=jnp.float32)


def attend(query, keys, values, segment):
    tokens = query.shape[0]
    block = min(512, tokens)
    scale = 1.0 / math.sqrt(HD)
    order = jnp.arange(tokens)
    outputs = []
    for first in range(0, tokens, block):
        last = first + block
        scores = (
            jnp.einsum(
                "qhd,khd->hqk", query[first:last], keys[:last], preferred_element_type=jnp.float32
            )
            * scale
        )
        allowed = (segment[first:last, None] == segment[None, :last]) & (
            order[None, :last] <= order[first:last, None]
        )
        top = jnp.max(jnp.where(allowed[None], scores, -1e30), axis=-1, keepdims=True)
        weights = jnp.exp(jnp.where(allowed[None], scores - top, -1e30))
        total = jnp.sum(weights, axis=-1)
        mixed = jnp.einsum(
            "hqk,khd->qhd",
            weights.astype(jnp.bfloat16),
            values[:last],
            preferred_element_type=jnp.float32,
        )
        outputs.append((mixed / jnp.transpose(total)[:, :, None]).astype(jnp.bfloat16))
    return jnp.concatenate(outputs, axis=0).reshape(tokens, -1)


def write_cache(keys, values, page_table):
    tokens = keys.shape[0]
    width = keys.shape[1] * keys.shape[2]
    pages = page_table.shape[0]
    page_size = tokens // pages
    owners = lax.axis_size("dp")
    per_owner = pages // owners
    me = lax.axis_index("dp")
    base = 128
    stacked = jnp.stack([keys.reshape(tokens, width), values.reshape(tokens, width)], axis=0)
    stacked = stacked.reshape(2, pages, page_size, width).transpose(1, 0, 2, 3)
    order = jnp.argsort(page_table // pages, stable=True)
    sorted_ids = page_table[order].reshape(owners, per_owner)
    code = jnp.stack([sorted_ids // base, sorted_ids % base], axis=-1).astype(jnp.bfloat16)
    slab = jnp.zeros((owners, 1, 2, page_size, width), jnp.bfloat16)
    slab = slab.at[:, 0, 0, 0, : 2 * per_owner].set(code.reshape(owners, 2 * per_owner))
    outgoing = jnp.concatenate(
        [stacked[order].reshape(owners, per_owner, 2, page_size, width), slab], axis=1
    )
    arrived = lax.all_to_all(outgoing, "dp", split_axis=0, concat_axis=0, tiled=True)
    codes = arrived[:, per_owner, 0, 0, : 2 * per_owner].astype(jnp.int32)
    codes = codes.reshape(owners, per_owner, 2)
    local = (codes[..., 0] * base + codes[..., 1] - me * pages).reshape(-1)
    empty = jnp.zeros((pages, 2, page_size, width), jnp.bfloat16)
    return empty.at[local].set(arrived[:, :per_owner].reshape(pages, 2, page_size, width))


def gather_packed(pieces, axis_name):
    rows = [piece.shape[0] for piece in pieces]
    packed = jnp.concatenate(pieces, axis=0)
    gathered = lax.all_gather(packed, axis_name, axis=0, tiled=False)
    outputs, first = [], 0
    for count in rows:
        outputs.append(gathered[:, first:first + count])
        first += count
    return outputs


def gather_rows(rows, axis_name):
    count = lax.axis_size(axis_name)
    copies = jnp.broadcast_to(rows[None], (count,) + rows.shape)
    gathered = lax.all_to_all(copies, axis_name, 0, 0, tiled=True)
    return gathered.reshape(count * rows.shape[0], rows.shape[1])


def sum_rows(terms, axis_name):
    count = lax.axis_size(axis_name)
    arrived = lax.all_to_all(
        terms.reshape(count, terms.shape[0] // count, terms.shape[1]), axis_name, 0, 0, tiled=True
    )
    return jnp.sum(arrived.astype(jnp.float32), axis=0)


def body(stream, segment, position, w_qkv, w_out, w_gate_up, w_down, page_table):
    tok_group = segment.shape[0]
    share_rows = stream.shape[0]
    local_cols = w_qkv.shape[2]
    attn_w = lax.all_gather(
        jnp.concatenate([w_qkv, jnp.transpose(w_out)[None]], axis=0), "dp", axis=1, tiled=True
    )
    mlp_w = lax.all_gather(
        jnp.concatenate([w_gate_up, jnp.transpose(w_down)[None]], axis=0), "dp", axis=1, tiled=True
    )
    full_stream = gather_rows(stream, "tensor")
    normed = layer_norm(full_stream).astype(jnp.bfloat16)
    local_heads = local_cols // HD
    projected = jnp.einsum("td,cdf->ctf", normed, attn_w[:3], preferred_element_type=jnp.float32)
    query = rotate(projected[0].reshape(tok_group, local_heads, HD), position).astype(jnp.bfloat16)
    keys = rotate(projected[1].reshape(tok_group, local_heads, HD), position).astype(jnp.bfloat16)
    values = projected[2].reshape(tok_group, local_heads, HD).astype(jnp.bfloat16)
    kv_cache = write_cache(keys, values, page_table)
    context = attend(query, keys, values, segment)
    attn_part = jnp.einsum("tr,dr->td", context, attn_w[3], preferred_element_type=jnp.float32)
    attn_part, kv_cache = lax.optimization_barrier((attn_part.astype(jnp.bfloat16), kv_cache))
    attn_mine = sum_rows(attn_part, "tensor")
    mid = (stream.astype(jnp.float32) + attn_mine).astype(jnp.bfloat16)
    normed2_mine = layer_norm(mid).astype(jnp.bfloat16)
    pieces = 2
    piece = share_rows // pieces
    mlp_pieces = []
    for first in range(0, share_rows, piece):
        rows = gather_rows(normed2_mine[first:first + piece], "tensor")
        gate_up = jnp.einsum("td,cdf->ctf", rows, mlp_w[:2], preferred_element_type=jnp.float32)
        hidden = (jax.nn.silu(gate_up[0]) * gate_up[1]).astype(jnp.bfloat16)
        mlp_part = jnp.einsum("tf,df->td", hidden, mlp_w[2], preferred_element_type=jnp.float32)
        mlp_pieces.append(sum_rows(mlp_part.astype(jnp.bfloat16), "tensor"))
    mlp_mine = jnp.concatenate(mlp_pieces, axis=0)
    layer_out = (mid.astype(jnp.float32) + mlp_mine).astype(jnp.bfloat16)
    return (layer_out, kv_cache)


def solution(mesh):
    return jax.shard_map(
        body,
        mesh=mesh,
        in_specs=(
            P(("dp", "tensor"), None),
            P("dp"),
            P("dp"),
            P(None, "dp", "tensor"),
            P("tensor", "dp"),
            P(None, "dp", "tensor"),
            P("tensor", "dp"),
            P("dp"),
        ),
        out_specs=(P(("dp", "tensor"), None), P("dp", None, None, "tensor")),
        check_vma=False,
    )
```
